32 devices in a mesh: brick: 16 (over z, y, x), view: 2 (over core).
Axes of the slice: x: 2, y: 2, z: 4, core: 2. Of those that a mesh axis runs over, the one named last changes fastest.
Arguments:
- tiles: float32 [2, 224, 25600], P('view', 'brick'), may hold values from -6 to 6
- shifts: int32 [2, 2, 224], P(None, 'view', 'brick'), may hold values from 0 to 16
- footprint: int32 [2, 16, 16, 2], P('view', 'brick'), may hold values from -1 to 13, as said below
- target: int32 [2, 224], P('view', 'brick'), may hold values from 0 to 27, as said below
Outputs:
- joined: float32 [448, 128, 128], P('brick', 'view')
The draws below stay inside these ranges and needn't reach their ends.
Inputs may be any that keep to these rules, and one draw needn't show every extreme that they name: footprint[v, s, d, c] is the local index of a tile of view v on brick index s that goes to owner d in slot c, or -1 for an empty slot; every one of the 14 tiles of (v, s) stands exactly once; each (v, s) sends exactly 2 tiles to each of 7 owners and none to the others. `target`: the tiles of one view that reach one owner have distinct targets; in each view some owner receives 28 tiles.
All inputs are finite; a program needn't handle non-finite values.
Results may differ from the reference program's by a relative error of at most 0.00011.
Values sent between devices are 32-bit elements; how exact they have to be, the bound alone decides.
No kernel may reach another device: no remote copies, remote signals or barrier semaphores. Data moves between devices by JAX's collectives and lax.ppermute only.
A program may use at most 64 MiB of HBM per device.

```python
import jax
import jax.numpy as jnp
from jax import lax

BS = 128
SHIFT = 8
BLUR = 4
SMOOTH = 4
CAP = 2
TILES_DEV = 14
BRICKS_DEV = 28
WIN = 144
EDGE = 160
NT = 224
NB = 448
N_BRICK = 16
N_VIEW = 2


def footprint_tables(key):
    base = jax.random.fold_in(key, 11)

    def one_view(view_key):
        key_perm, key_rot, key_brick = jax.random.split(view_key, 3)
        order = jax.random.permutation(key_perm, N_BRICK)
        rotate = jax.random.randint(key_rot, (), 0, N_BRICK)
        start = (rotate + order // 2) % N_BRICK
        groups = TILES_DEV // CAP
        owner_ids = jnp.arange(N_BRICK)
        step_of = (owner_ids[None, :] - start[:, None]) % N_BRICK
        slot_ids = jnp.arange(CAP)
        listed = jnp.where((step_of < groups)[:, :, None], step_of[:, :, None] * CAP + slot_ids[None, None, :], -1)
        tile_ids = jnp.arange(TILES_DEV)
        group_of = tile_ids // CAP
        slot_of = tile_ids % CAP
        local_ids = CAP * (2 * group_of[None, :] + (order % 2)[:, None]) + slot_of[None, :]
        mixing = jax.random.permutation(key_brick, BRICKS_DEV)
        targets = mixing[local_ids]
        return (listed.astype(jnp.int32), targets.reshape(-1).astype(jnp.int32))
    view_keys = jax.random.split(base, N_VIEW)
    return jax.vmap(one_view)(view_keys)


def draw_footprint(key, part):
    return footprint_tables(key)[0]


def draw_target(key, part):
    return footprint_tables(key)[1]


def plant(drawn, stream_key, smallest, largest):
    extent = drawn.shape
    index_at = [jax.random.randint(jax.random.fold_in(stream_key, axis), (), 0, extent[axis]) for axis in range(len(extent))]
    drawn = drawn.at[tuple(index_at)].set(smallest)
    longest = extent.index(max(extent))
    index_at[longest] = (index_at[longest] + 1) % extent[longest]
    return drawn.at[tuple(index_at)].set(largest)


def shard_levels(rng, extent, pieces, low, high):
    level = 1.0
    for dim, shards_of in pieces:
        heights = jax.random.uniform(jax.random.fold_in(jax.random.fold_in(rng, 6), dim), (shards_of,), jnp.float32, low / len(pieces), high / len(pieces))
        level = level * jnp.repeat(jnp.exp(heights), extent[dim] // shards_of).reshape((-1,) + (1,) * (len(extent) - 1 - dim))
    return level


def bell_draw(own_key, dims, spread, most, shards=(), kind=jnp.bfloat16):
    drawn = jax.random.normal(own_key, dims, jnp.float32) * spread
    if len(shards) > 0:
        drawn = shard_levels(own_key, dims, shards, -0.22, 0.18) * drawn
    return jnp.clip(drawn, min=-most, max=most).astype(kind)


def setup_inputs(seed: int = 0) -> dict:
    streams_of = jax.random.split(jax.random.key(seed), 5)
    return {
        "tiles": bell_draw(streams_of[0], (N_VIEW, NT, EDGE * EDGE), 1.0, 6.0, ((0, 2), (1, 16)), jnp.float32),
        "shifts": plant(jax.random.randint(streams_of[1], (2, N_VIEW, NT), 0, 2 * SHIFT + 1), jax.random.fold_in(streams_of[1], 1), 0, 2 * SHIFT).astype(jnp.int32),
        "footprint": draw_footprint(jax.random.fold_in(streams_of[4], 71), 0),
        "target": draw_target(jax.random.fold_in(streams_of[4], 71), 0),
    }


def blur_matrix(out_len, radius):
    out_index = jnp.arange(out_len)[:, None]
    in_index = jnp.arange(out_len + 2 * radius)[None, :]
    offset = (in_index - out_index - radius).astype(jnp.float32)
    spread_px = radius / 2.0
    tap_values = jnp.exp(-offset * offset / (2.0 * spread_px * spread_px))
    tap_line = jnp.arange(-radius, radius + 1).astype(jnp.float32)
    tap_sum = jnp.sum(jnp.exp(-tap_line * tap_line / (2.0 * spread_px * spread_px)))
    inside = jnp.abs(offset) <= radius
    return jnp.where(inside, tap_values / tap_sum, jnp.zeros_like(tap_values)).astype(jnp.float32)


def contrast(windows):
    inner_len = WIN - 2 * BLUR
    highest = lax.Precision.HIGHEST
    first_blur = blur_matrix(inner_len, BLUR)
    second_blur = blur_matrix(BS, SMOOTH)
    row_pass = jnp.einsum('ow,nwv->nov', first_blur, windows, precision=highest)
    local_mean = jnp.einsum('nov,pv->nop', row_pass, first_blur, precision=highest)
    inner_part = windows[:, BLUR:BLUR + inner_len, BLUR:BLUR + inner_len]
    energy = (inner_part - local_mean) ** 2
    row_two = jnp.einsum('ow,nwv->nov', second_blur, energy, precision=highest)
    weight = jnp.einsum('nov,pv->nop', row_two, second_blur, precision=highest)
    margin = BLUR + SMOOTH
    center = windows[:, margin:margin + BS, margin:margin + BS]
    return weight * center, weight


def cut_window(one_tile, shift_row, shift_col):
    square_tile = one_tile.reshape(EDGE, EDGE)
    return lax.dynamic_slice(square_tile, (shift_row, shift_col), (WIN, WIN))


def reference(tiles, shifts, footprint, target):
    tile_ids = jnp.arange(TILES_DEV).astype(jnp.int32)
    listed = footprint[..., None] == tile_ids
    owner_ids = jnp.arange(N_BRICK).astype(jnp.int32)
    owner_of = jnp.sum(jnp.where(listed, owner_ids[None, None, :, None, None], 0), axis=(2, 3)).astype(jnp.int32)
    owner_of = owner_of.reshape(N_VIEW, N_BRICK * TILES_DEV)
    brick_of = (owner_of * BRICKS_DEV + target).astype(jnp.int32)
    start_sums = (jnp.zeros((NB, BS, BS), jnp.float32), jnp.zeros((NB, BS, BS), jnp.float32))

    def per_view(running, inputs):
        view_tiles, shift_row, shift_col, view_bricks = inputs
        windows = jax.vmap(cut_window)(view_tiles, shift_row, shift_col)
        weighted, weights = contrast(windows)
        return (running[0].at[view_bricks].add(weighted), running[1].at[view_bricks].add(weights)), None

    (numer, denom), _ = lax.scan(per_view, start_sums, (tiles, shifts[0], shifts[1], brick_of))
    return numer / jnp.maximum(denom, 1.0)
```

```python
import jax
import jax.numpy as jnp
from jax import lax
from jax.sharding import PartitionSpec as P

BS = 128
BLUR = 4
SMOOTH = 4
BRICKS_DEV = 28
WIN = 144
EDGE = 160


def blur_matrix(out_len, radius):
    out_index = jnp.arange(out_len)[:, None]
    in_index = jnp.arange(out_len + 2 * radius)[None, :]
    offset = (in_index - out_index - radius).astype(jnp.float32)
    spread_px = radius / 2.0
    tap_values = jnp.exp(-offset * offset / (2.0 * spread_px * spread_px))
    tap_line = jnp.arange(-radius, radius + 1).astype(jnp.float32)
    tap_sum = jnp.sum(jnp.exp(-tap_line * tap_line / (2.0 * spread_px * spread_px)))
    inside = jnp.abs(offset) <= radius
    return jnp.where(inside, tap_values / tap_sum, jnp.zeros_like(tap_values))


def contrast(windows):
    inner_len = WIN - 2 * BLUR
    highest = lax.Precision.HIGHEST
    first_blur = blur_matrix(inner_len, BLUR)
    second_blur = blur_matrix(BS, SMOOTH)
    row_pass = jnp.einsum("ow,nwv->nov", first_blur, windows, precision=highest)
    local_mean = jnp.einsum("nov,pv->nop", row_pass, first_blur, precision=highest)
    inner_part = windows[:, BLUR : BLUR + inner_len, BLUR : BLUR + inner_len]
    energy = (inner_part - local_mean) ** 2
    row_two = jnp.einsum("ow,nwv->nov", second_blur, energy, precision=highest)
    weight = jnp.einsum("nov,pv->nop", row_two, second_blur, precision=highest)
    margin = BLUR + SMOOTH
    center = windows[:, margin : margin + BS, margin : margin + BS]
    return (weight * center, weight)


def cut_windows(square, shift_row, shift_col):
    highest = lax.Precision.HIGHEST
    span = jnp.arange(WIN)[None, :, None]
    cells = jnp.arange(EDGE)[None, None, :]
    pick_rows = (span + shift_row[:, None, None] == cells).astype(jnp.float32)
    pick_cols = (span + shift_col[:, None, None] == cells).astype(jnp.float32)
    rows_cut = jnp.einsum("nie,nef->nif", pick_rows, square, precision=highest)
    return jnp.einsum("nif,njf->nij", rows_cut, pick_cols, precision=highest)


def arrange_slots(arrived, labels):
    flat_slots = arrived.reshape((-1,) + arrived.shape[2:])
    label_ids = labels.reshape(-1).astype(jnp.int32)
    matches = (label_ids[:, None] == jnp.arange(BRICKS_DEV)[None, :]).astype(jnp.int32)
    slot_of = jnp.argmax(matches, axis=0)
    present = jnp.max(matches, axis=0).astype(jnp.float32)
    return flat_slots[slot_of] * present[:, None, None]


def local(tiles, shifts, footprint, target):
    count = tiles.shape[1]
    square = tiles.reshape(count, EDGE, EDGE)
    windows = cut_windows(square, shifts[0, 0], shifts[1, 0])
    slot_list = footprint[0, 0]
    filled = slot_list >= 0
    picked = jnp.maximum(slot_list, 0)
    labels = jnp.where(filled, target[0][picked], -1).astype(jnp.float32)
    slot_mask = filled.astype(jnp.float32)[:, :, None, None]
    packed = windows[picked] * slot_mask
    arrived, arrived_labels = (
        lax.all_to_all(packed, "brick", split_axis=0, concat_axis=0, tiled=True),
        lax.all_to_all(labels, "brick", split_axis=0, concat_axis=0, tiled=True),
    )
    arranged = arrange_slots(arrived, arrived_labels)
    weighted, weights = contrast(arranged)
    numer, denom = (
        lax.psum_scatter(weighted, "view", scatter_dimension=1, tiled=True),
        lax.psum_scatter(weights, "view", scatter_dimension=1, tiled=True),
    )
    return numer / jnp.maximum(denom, 1.0)


def solution(mesh):
    placed = (
        P("view", "brick", None),
        P(None, "view", "brick"),
        P("view", "brick", None, None),
        P("view", "brick"),
    )
    return jax.shard_map(
        local, mesh=mesh, in_specs=placed, out_specs=P("brick", "view", None), check_vma=False
    )
```

```python
import functools

import jax
import jax.numpy as jnp
from jax import lax
from jax.sharding import PartitionSpec as P

BS = 128
BLUR = 4
SMOOTH = 4
BRICKS_DEV = 28
WIN = 144
EDGE = 160


def blur_matrix(out_len, radius):
    out_index = jnp.arange(out_len)[:, None]
    in_index = jnp.arange(out_len + 2 * radius)[None, :]
    offset = (in_index - out_index - radius).astype(jnp.float32)
    spread_px = radius / 2.0
    tap_values = jnp.exp(-offset * offset / (2.0 * spread_px * spread_px))
    tap_line = jnp.arange(-radius, radius + 1).astype(jnp.float32)
    tap_sum = jnp.sum(jnp.exp(-tap_line * tap_line / (2.0 * spread_px * spread_px)))
    inside = jnp.abs(offset) <= radius
    return jnp.where(inside, tap_values / tap_sum, jnp.zeros_like(tap_values))


def contrast(windows):
    inner_len = WIN - 2 * BLUR
    highest = lax.Precision.HIGHEST
    first_blur = blur_matrix(inner_len, BLUR)
    second_blur = blur_matrix(BS, SMOOTH)
    row_pass = jnp.einsum("ow,nwv->nov", first_blur, windows, precision=highest)
    local_mean = jnp.einsum("nov,pv->nop", row_pass, first_blur, precision=highest)
    inner_part = windows[:, BLUR : BLUR + inner_len, BLUR : BLUR + inner_len]
    energy = (inner_part - local_mean) ** 2
    row_two = jnp.einsum("ow,nwv->nov", second_blur, energy, precision=highest)
    weight = jnp.einsum("nov,pv->nop", row_two, second_blur, precision=highest)
    margin = BLUR + SMOOTH
    center = windows[:, margin : margin + BS, margin : margin + BS]
    return (weight * center, weight)


def cut_windows(square, shift_row, shift_col):
    highest = lax.Precision.HIGHEST
    span = jnp.arange(WIN)[None, :, None]
    cells = jnp.arange(EDGE)[None, None, :]
    pick_rows = (span + shift_row[:, None, None] == cells).astype(jnp.float32)
    pick_cols = (span + shift_col[:, None, None] == cells).astype(jnp.float32)
    rows_cut = jnp.einsum("nie,nef->nif", pick_rows, square, precision=highest)
    return jnp.einsum("nif,njf->nij", rows_cut, pick_cols, precision=highest)


def arrange_slots(arrived, labels):
    flat_slots = arrived.reshape((-1,) + arrived.shape[2:])
    label_ids = labels.reshape(-1).astype(jnp.int32)
    matches = (label_ids[:, None] == jnp.arange(BRICKS_DEV)[None, :]).astype(jnp.int32)
    slot_of = jnp.argmax(matches, axis=0)
    present = jnp.max(matches, axis=0).astype(jnp.float32)
    return flat_slots[slot_of] * present[:, None, None]


def swap_halves(part):
    me = lax.axis_index("view")
    halves = part.reshape(part.shape[0], 2, part.shape[1] // 2, part.shape[2])
    kept = lax.dynamic_index_in_dim(halves, me, axis=1, keepdims=False)
    outgoing = lax.dynamic_index_in_dim(halves, 1 - me, axis=1, keepdims=False)
    arrived = lax.ppermute(outgoing, "view", perm=[(0, 1), (1, 0)])
    return kept + arrived


def local(n_view, tiles, shifts, footprint, target):
    count = tiles.shape[1]
    square = tiles.reshape(count, EDGE, EDGE)
    windows = cut_windows(square, shifts[0, 0], shifts[1, 0])
    slot_list = footprint[0, 0]
    filled = slot_list >= 0
    picked = jnp.maximum(slot_list, 0)
    labels = jnp.where(filled, target[0][picked], -1).astype(jnp.float32)
    slot_mask = filled.astype(jnp.float32)[:, :, None, None]
    packed = windows[picked] * slot_mask
    arrived, arrived_labels = (
        lax.all_to_all(packed, "brick", split_axis=0, concat_axis=0, tiled=True),
        lax.all_to_all(labels, "brick", split_axis=0, concat_axis=0, tiled=True),
    )
    arranged = arrange_slots(arrived, arrived_labels)
    weighted, weights = contrast(arranged)
    if n_view == 2:
        numer, denom = swap_halves(weighted), swap_halves(weights)
    else:
        numer, denom = (
            lax.psum_scatter(weighted, "view", scatter_dimension=1, tiled=True),
            lax.psum_scatter(weights, "view", scatter_dimension=1, tiled=True),
        )
    return numer / jnp.maximum(denom, 1.0)


def solution(mesh):
    placed = (
        P("view", "brick", None),
        P(None, "view", "brick"),
        P("view", "brick", None, None),
        P("view", "brick"),
    )
    return jax.shard_map(
        functools.partial(local, mesh.shape["view"]), mesh=mesh, in_specs=placed, out_specs=P("brick", "view", None), check_vma=False
    )
```

```python
import functools

import jax
import jax.numpy as jnp
from jax import lax
from jax.sharding import PartitionSpec as P

BS = 128
BLUR = 4
SMOOTH = 4
BRICKS_DEV = 28
WIN = 144
EDGE = 160
LANES = 128


def blur_matrix(out_len, radius):
    out_index = jnp.arange(out_len)[:, None]
    in_index = jnp.arange(out_len + 2 * radius)[None, :]
    offset = (in_index - out_index - radius).astype(jnp.float32)
    spread_px = radius / 2.0
    tap_values = jnp.exp(-offset * offset / (2.0 * spread_px * spread_px))
    tap_line = jnp.arange(-radius, radius + 1).astype(jnp.float32)
    tap_sum = jnp.sum(jnp.exp(-tap_line * tap_line / (2.0 * spread_px * spread_px)))
    inside = jnp.abs(offset) <= radius
    return jnp.where(inside, tap_values / tap_sum, jnp.zeros_like(tap_values))


def contrast(windows):
    inner_len = WIN - 2 * BLUR
    highest = lax.Precision.HIGHEST
    first_blur = blur_matrix(inner_len, BLUR)
    second_blur = blur_matrix(BS, SMOOTH)
    row_pass = jnp.einsum("ow,nwv->nov", first_blur, windows, precision=highest)
    local_mean = jnp.einsum("nov,pv->nop", row_pass, first_blur, precision=highest)
    inner_part = windows[:, BLUR : BLUR + inner_len, BLUR : BLUR + inner_len]
    energy = (inner_part - local_mean) ** 2
    row_two = jnp.einsum("ow,nwv->nov", second_blur, energy, precision=highest)
    weight = jnp.einsum("nov,pv->nop", row_two, second_blur, precision=highest)
    margin = BLUR + SMOOTH
    center = windows[:, margin : margin + BS, margin : margin + BS]
    return (weight * center, weight)


def cut_windows(square, shift_row, shift_col):
    highest = lax.Precision.HIGHEST
    span = jnp.arange(WIN)[None, :, None]
    cells = jnp.arange(EDGE)[None, None, :]
    pick_rows = (span + shift_row[:, None, None] == cells).astype(jnp.float32)
    pick_cols = (span + shift_col[:, None, None] == cells).astype(jnp.float32)
    rows_cut = jnp.einsum("nie,nef->nif", pick_rows, square, precision=highest)
    return jnp.einsum("nif,njf->nij", rows_cut, pick_cols, precision=highest)


def arrange_slots(arrived, labels):
    flat_slots = arrived.reshape((-1,) + arrived.shape[2:])
    label_ids = labels.reshape(-1).astype(jnp.int32)
    matches = (label_ids[:, None] == jnp.arange(BRICKS_DEV)[None, :]).astype(jnp.int32)
    slot_of = jnp.argmax(matches, axis=0)
    present = jnp.max(matches, axis=0).astype(jnp.float32)
    return flat_slots[slot_of] * present[:, None, None]


def swap_halves(part):
    me = lax.axis_index("view")
    halves = part.reshape(part.shape[0], 2, part.shape[1] // 2, part.shape[2])
    kept = lax.dynamic_index_in_dim(halves, me, axis=1, keepdims=False)
    outgoing = lax.dynamic_index_in_dim(halves, 1 - me, axis=1, keepdims=False)
    arrived = lax.ppermute(outgoing, "view", perm=[(0, 1), (1, 0)])
    return kept + arrived


def local(n_view, tiles, shifts, footprint, target):
    count = tiles.shape[1]
    square = tiles.reshape(count, EDGE, EDGE)
    windows = cut_windows(square, shifts[0, 0], shifts[1, 0])
    slot_list = footprint[0, 0]
    filled = slot_list >= 0
    picked = jnp.maximum(slot_list, 0)
    labels = jnp.where(filled, target[0][picked], -1).astype(jnp.float32)
    slot_mask = filled.astype(jnp.float32)[:, :, None, None]
    owners, cap = slot_list.shape
    dense_rows = WIN * WIN // LANES
    packed = (windows[picked] * slot_mask).reshape(owners, cap, dense_rows, LANES)
    label_row = jnp.broadcast_to(labels[:, :, None, None], (owners, cap, 1, LANES))
    payload = jnp.concatenate([packed, label_row], axis=2)
    payload = payload.reshape(owners, cap * (dense_rows + 1), LANES)
    arrived = lax.all_to_all(payload, "brick", split_axis=0, concat_axis=0, tiled=True)
    arrived = arrived.reshape(owners, cap, dense_rows + 1, LANES)
    arrived_labels = arrived[:, :, dense_rows, 0]
    arrived = arrived[:, :, :dense_rows].reshape(owners, cap, WIN, WIN)
    arranged = arrange_slots(arrived, arrived_labels)
    weighted, weights = contrast(arranged)
    if n_view == 2:
        numer, denom = swap_halves(weighted), swap_halves(weights)
    else:
        numer, denom = (
            lax.psum_scatter(weighted, "view", scatter_dimension=1, tiled=True),
            lax.psum_scatter(weights, "view", scatter_dimension=1, tiled=True),
        )
    return numer / jnp.maximum(denom, 1.0)


def solution(mesh):
    placed = (
        P("view", "brick", None),
        P(None, "view", "brick"),
        P("view", "brick", None, None),
        P("view", "brick"),
    )
    return jax.shard_map(
        functools.partial(local, mesh.shape["view"]), mesh=mesh, in_specs=placed, out_specs=P("brick", "view", None), check_vma=False
    )
```

```python
import functools

import jax
import jax.numpy as jnp
from jax import lax
from jax.sharding import PartitionSpec as P

BS = 128
BLUR = 4
SMOOTH = 4
BRICKS_DEV = 28
WIN = 144
EDGE = 160
LANES = 128


def blur_matrix(out_len, radius):
    out_index = jnp.arange(out_len)[:, None]
    in_index = jnp.arange(out_len + 2 * radius)[None, :]
    offset = (in_index - out_index - radius).astype(jnp.float32)
    spread_px = radius / 2.0
    tap_values = jnp.exp(-offset * offset / (2.0 * spread_px * spread_px))
    tap_line = jnp.arange(-radius, radius + 1).astype(jnp.float32)
    tap_sum = jnp.sum(jnp.exp(-tap_line * tap_line / (2.0 * spread_px * spread_px)))
    inside = jnp.abs(offset) <= radius
    return jnp.where(inside, tap_values / tap_sum, jnp.zeros_like(tap_values))


def contrast(windows):
    inner_len = WIN - 2 * BLUR
    highest = lax.Precision.HIGHEST
    first_blur = blur_matrix(inner_len, BLUR)
    second_blur = blur_matrix(BS, SMOOTH)
    row_pass = jnp.einsum("ow,nwv->nov", first_blur, windows, precision=highest)
    local_mean = jnp.einsum("nov,pv->nop", row_pass, first_blur, precision=highest)
    inner_part = windows[:, BLUR : BLUR + inner_len, BLUR : BLUR + inner_len]
    energy = (inner_part - local_mean) ** 2
    row_two = jnp.einsum("ow,nwv->nov", second_blur, energy, precision=highest)
    weight = jnp.einsum("nov,pv->nop", row_two, second_blur, precision=highest)
    margin = BLUR + SMOOTH
    center = windows[:, margin : margin + BS, margin : margin + BS]
    return (weight * center, weight)


def cut_windows(square, shift_row, shift_col):
    highest = lax.Precision.HIGHEST
    span = jnp.arange(WIN)[None, :, None]
    cells = jnp.arange(EDGE)[None, None, :]
    pick_rows = (span + shift_row[:, None, None] == cells).astype(jnp.float32)
    pick_cols = (span + shift_col[:, None, None] == cells).astype(jnp.float32)
    rows_cut = jnp.einsum("nie,nef->nif", pick_rows, square, precision=highest)
    return jnp.einsum("nif,njf->nij", rows_cut, pick_cols, precision=highest)


def arrange_slots(arrived, labels):
    flat_slots = arrived.reshape((-1,) + arrived.shape[2:])
    label_ids = labels.reshape(-1).astype(jnp.int32)
    matches = (label_ids[:, None] == jnp.arange(BRICKS_DEV)[None, :]).astype(jnp.int32)
    slot_of = jnp.argmax(matches, axis=0)
    present = jnp.max(matches, axis=0).astype(jnp.float32)
    return flat_slots[slot_of] * present[:, None, None]


def swap_halves(part):
    me = lax.axis_index("view")
    halves = part.reshape(part.shape[0], 2, part.shape[1] // 2, part.shape[2])
    kept = lax.dynamic_index_in_dim(halves, me, axis=1, keepdims=False)
    outgoing = lax.dynamic_index_in_dim(halves, 1 - me, axis=1, keepdims=False)
    arrived = lax.ppermute(outgoing, "view", perm=[(0, 1), (1, 0)])
    return kept + arrived


def local(n_view, tiles, shifts, footprint, target):
    count = tiles.shape[1]
    square = tiles.reshape(count, EDGE, EDGE)
    windows = cut_windows(square, shifts[0, 0], shifts[1, 0])
    slot_list = footprint[0, 0]
    filled = slot_list >= 0
    picked = jnp.maximum(slot_list, 0)
    labels = jnp.where(filled, target[0][picked], -1).astype(jnp.float32)
    owners, cap = slot_list.shape
    dense_rows = WIN * WIN // LANES
    bricks = jnp.arange(BRICKS_DEV)
    weighted = weights = None
    for slot in range(cap):
        mask = filled[:, slot].astype(jnp.float32)[:, None, None]
        packed = (windows[picked[:, slot]] * mask).reshape(owners, dense_rows, LANES)
        label_row = jnp.broadcast_to(labels[:, slot, None, None], (owners, 1, LANES))
        payload = jnp.concatenate([packed, label_row], axis=1)
        arrived = lax.all_to_all(payload, "brick", split_axis=0, concat_axis=0, tiled=True)
        arrived_labels = arrived[:, dense_rows, 0].astype(jnp.int32)
        slots = arrived[:, :dense_rows].reshape(owners, WIN, WIN)
        slot_weighted, slot_weights = contrast(slots)
        place = (arrived_labels[None, :] == bricks[:, None]).astype(jnp.float32)
        highest = lax.Precision.HIGHEST
        placed_weighted = jnp.einsum("bs,sij->bij", place, slot_weighted, precision=highest)
        placed_weights = jnp.einsum("bs,sij->bij", place, slot_weights, precision=highest)
        if weighted is None:
            weighted, weights = placed_weighted, placed_weights
        else:
            weighted, weights = weighted + placed_weighted, weights + placed_weights
    if n_view == 2:
        numer, denom = swap_halves(weighted), swap_halves(weights)
    else:
        numer, denom = (
            lax.psum_scatter(weighted, "view", scatter_dimension=1, tiled=True),
            lax.psum_scatter(weights, "view", scatter_dimension=1, tiled=True),
        )
    return numer / jnp.maximum(denom, 1.0)


def solution(mesh):
    placed = (
        P("view", "brick", None),
        P(None, "view", "brick"),
        P("view", "brick", None, None),
        P("view", "brick"),
    )
    return jax.shard_map(
        functools.partial(local, mesh.shape["view"]), mesh=mesh, in_specs=placed, out_specs=P("brick", "view", None), check_vma=False
    )
```

```python
import functools

import jax
import jax.numpy as jnp
from jax import lax
from jax.sharding import PartitionSpec as P

BS = 128
BLUR = 4
SMOOTH = 4
BRICKS_DEV = 28
WIN = 144
EDGE = 160
LANES = 128


def blur_matrix(out_len, radius):
    out_index = jnp.arange(out_len)[:, None]
    in_index = jnp.arange(out_len + 2 * radius)[None, :]
    offset = (in_index - out_index - radius).astype(jnp.float32)
    spread_px = radius / 2.0
    tap_values = jnp.exp(-offset * offset / (2.0 * spread_px * spread_px))
    tap_line = jnp.arange(-radius, radius + 1).astype(jnp.float32)
    tap_sum = jnp.sum(jnp.exp(-tap_line * tap_line / (2.0 * spread_px * spread_px)))
    inside = jnp.abs(offset) <= radius
    return jnp.where(inside, tap_values / tap_sum, jnp.zeros_like(tap_values))


def contrast(windows):
    inner_len = WIN - 2 * BLUR
    highest = lax.Precision.HIGH
    first_blur = blur_matrix(inner_len, BLUR)
    second_blur = blur_matrix(BS, SMOOTH)
    row_pass = jnp.einsum("ow,nwv->nov", first_blur, windows, precision=highest)
    local_mean = jnp.einsum("nov,pv->nop", row_pass, first_blur, precision=highest)
    inner_part = windows[:, BLUR : BLUR + inner_len, BLUR : BLUR + inner_len]
    energy = (inner_part - local_mean) ** 2
    row_two = jnp.einsum("ow,nwv->nov", second_blur, energy, precision=highest)
    weight = jnp.einsum("nov,pv->nop", row_two, second_blur, precision=highest)
    margin = BLUR + SMOOTH
    center = windows[:, margin : margin + BS, margin : margin + BS]
    return (weight * center, weight)


def cut_windows(square, shift_row, shift_col):
    highest = lax.Precision.HIGHEST
    span = jnp.arange(WIN)[None, :, None]
    cells = jnp.arange(EDGE)[None, None, :]
    pick_rows = (span + shift_row[:, None, None] == cells).astype(jnp.float32)
    pick_cols = (span + shift_col[:, None, None] == cells).astype(jnp.float32)
    rows_cut = jnp.einsum("nie,nef->nif", pick_rows, square, precision=highest)
    return jnp.einsum("nif,njf->nij", rows_cut, pick_cols, precision=highest)


def arrange_slots(arrived, labels):
    flat_slots = arrived.reshape((-1,) + arrived.shape[2:])
    label_ids = labels.reshape(-1).astype(jnp.int32)
    matches = (label_ids[:, None] == jnp.arange(BRICKS_DEV)[None, :]).astype(jnp.int32)
    slot_of = jnp.argmax(matches, axis=0)
    present = jnp.max(matches, axis=0).astype(jnp.float32)
    return flat_slots[slot_of] * present[:, None, None]


def swap_halves(part):
    me = lax.axis_index("view")
    halves = part.reshape(part.shape[0], 2, part.shape[1] // 2, part.shape[2])
    kept = lax.dynamic_index_in_dim(halves, me, axis=1, keepdims=False)
    outgoing = lax.dynamic_index_in_dim(halves, 1 - me, axis=1, keepdims=False)
    arrived = lax.ppermute(outgoing, "view", perm=[(0, 1), (1, 0)])
    return kept + arrived


def local(n_view, tiles, shifts, footprint, target):
    count = tiles.shape[1]
    flat = lax.optimization_barrier(tiles.reshape(count, EDGE * EDGE // LANES, LANES))
    square = flat.reshape(count, EDGE, EDGE)
    windows = cut_windows(square, shifts[0, 0], shifts[1, 0])
    slot_list = footprint[0, 0]
    filled = slot_list >= 0
    picked = jnp.maximum(slot_list, 0)
    labels = jnp.where(filled, target[0][picked], -1).astype(jnp.float32)
    owners, cap = slot_list.shape
    dense_rows = WIN * WIN // LANES
    bricks = jnp.arange(BRICKS_DEV)
    weighted = weights = None
    for slot in range(cap):
        mask = filled[:, slot].astype(jnp.float32)[:, None, None]
        packed = (windows[picked[:, slot]] * mask).reshape(owners, dense_rows, LANES)
        label_row = jnp.broadcast_to(labels[:, slot, None, None], (owners, 1, LANES))
        payload = jnp.concatenate([packed, label_row], axis=1)
        arrived = lax.all_to_all(payload, "brick", split_axis=0, concat_axis=0, tiled=True)
        arrived_labels = arrived[:, dense_rows, 0].astype(jnp.int32)
        slots = arrived[:, :dense_rows].reshape(owners, WIN, WIN)
        slot_weighted, slot_weights = contrast(slots)
        place = (arrived_labels[None, :] == bricks[:, None]).astype(jnp.float32)
        highest = lax.Precision.HIGHEST
        placed_weighted = jnp.einsum("bs,sij->bij", place, slot_weighted, precision=highest)
        placed_weights = jnp.einsum("bs,sij->bij", place, slot_weights, precision=highest)
        if weighted is None:
            weighted, weights = placed_weighted, placed_weights
        else:
            weighted, weights = weighted + placed_weighted, weights + placed_weights
    if n_view == 2:
        numer, denom = swap_halves(weighted), swap_halves(weights)
    else:
        numer, denom = (
            lax.psum_scatter(weighted, "view", scatter_dimension=1, tiled=True),
            lax.psum_scatter(weights, "view", scatter_dimension=1, tiled=True),
        )
    return numer / jnp.maximum(denom, 1.0)


def solution(mesh):
    placed = (
        P("view", "brick", None),
        P(None, "view", "brick"),
        P("view", "brick", None, None),
        P("view", "brick"),
    )
    return jax.shard_map(
        functools.partial(local, mesh.shape["view"]), mesh=mesh, in_specs=placed, out_specs=P("brick", "view", None), check_vma=False
    )
```

```python
import functools

import jax
import jax.numpy as jnp
from jax import lax
from jax.sharding import PartitionSpec as P

BS = 128
BLUR = 4
SMOOTH = 4
BRICKS_DEV = 28
WIN = 144
EDGE = 160
LANES = 128


def blur_matrix(out_len, radius):
    out_index = jnp.arange(out_len)[:, None]
    in_index = jnp.arange(out_len + 2 * radius)[None, :]
    offset = (in_index - out_index - radius).astype(jnp.float32)
    spread_px = radius / 2.0
    tap_values = jnp.exp(-offset * offset / (2.0 * spread_px * spread_px))
    tap_line = jnp.arange(-radius, radius + 1).astype(jnp.float32)
    tap_sum = jnp.sum(jnp.exp(-tap_line * tap_line / (2.0 * spread_px * spread_px)))
    inside = jnp.abs(offset) <= radius
    return jnp.where(inside, tap_values / tap_sum, jnp.zeros_like(tap_values))


def contrast(windows):
    inner_len = WIN - 2 * BLUR
    highest = lax.Precision.HIGH
    first_blur = blur_matrix(inner_len, BLUR)
    second_blur = blur_matrix(BS, SMOOTH)
    row_pass = jnp.einsum("ow,nwv->nov", first_blur, windows, precision=highest)
    local_mean = jnp.einsum("nov,pv->nop", row_pass, first_blur, precision=highest)
    inner_part = windows[:, BLUR : BLUR + inner_len, BLUR : BLUR + inner_len]
    energy = (inner_part - local_mean) ** 2
    row_two = jnp.einsum("ow,nwv->nov", second_blur, energy, precision=highest)
    weight = jnp.einsum("nov,pv->nop", row_two, second_blur, precision=highest)
    margin = BLUR + SMOOTH
    center = windows[:, margin : margin + BS, margin : margin + BS]
    return (weight * center, weight)


def cut_windows(square, shift_row, shift_col):
    highest = lax.Precision.HIGHEST
    span = jnp.arange(WIN)[None, :, None]
    cells = jnp.arange(EDGE)[None, None, :]
    pick_rows = (span + shift_row[:, None, None] == cells).astype(jnp.float32)
    pick_cols = (span + shift_col[:, None, None] == cells).astype(jnp.float32)
    rows_cut = jnp.einsum("nie,nef->nif", pick_rows, square, precision=highest)
    return jnp.einsum("nif,njf->nij", rows_cut, pick_cols, precision=highest)


def arrange_slots(arrived, labels):
    flat_slots = arrived.reshape((-1,) + arrived.shape[2:])
    label_ids = labels.reshape(-1).astype(jnp.int32)
    matches = (label_ids[:, None] == jnp.arange(BRICKS_DEV)[None, :]).astype(jnp.int32)
    slot_of = jnp.argmax(matches, axis=0)
    present = jnp.max(matches, axis=0).astype(jnp.float32)
    return flat_slots[slot_of] * present[:, None, None]


def swap_halves(part):
    me = lax.axis_index("view")
    halves = part.reshape(part.shape[0], 2, part.shape[1] // 2, part.shape[2])
    kept = lax.dynamic_index_in_dim(halves, me, axis=1, keepdims=False)
    outgoing = lax.dynamic_index_in_dim(halves, 1 - me, axis=1, keepdims=False)
    arrived = lax.ppermute(outgoing, "view", perm=[(0, 1), (1, 0)])
    return kept + arrived


def local(n_view, tiles, shifts, footprint, target):
    count = tiles.shape[1]
    flat = lax.optimization_barrier(tiles.reshape(count, EDGE * EDGE // LANES, LANES))
    square = flat.reshape(count, EDGE, EDGE)
    windows = cut_windows(square, shifts[0, 0], shifts[1, 0])
    slot_list = footprint[0, 0]
    filled = slot_list >= 0
    picked = jnp.maximum(slot_list, 0)
    labels = jnp.where(filled, target[0][picked], -1).astype(jnp.float32)
    owners, cap = slot_list.shape
    dense_rows = WIN * WIN // LANES
    spill_rows = dense_rows - WIN
    bricks = jnp.arange(BRICKS_DEV)
    weighted = weights = None
    for slot in range(cap):
        mask = filled[:, slot].astype(jnp.float32)[:, None, None]
        picked_windows = windows[picked[:, slot]] * mask
        spill = picked_windows[:, :, LANES:].reshape(owners, spill_rows, LANES)
        label_row = jnp.broadcast_to(labels[:, slot, None, None], (owners, 1, LANES))
        payload = jnp.concatenate([picked_windows[:, :, :LANES], spill, label_row], axis=1)
        arrived = lax.all_to_all(payload, "brick", split_axis=0, concat_axis=0, tiled=True)
        if weighted is not None:
            weighted, weights, arrived = lax.optimization_barrier((weighted, weights, arrived))
        arrived_labels = arrived[:, dense_rows, 0].astype(jnp.int32)
        spill = arrived[:, WIN:dense_rows].reshape(owners, WIN, WIN - LANES)
        slots = jnp.concatenate([arrived[:, :WIN], spill], axis=2)
        slot_weighted, slot_weights = contrast(slots)
        place = (arrived_labels[None, :] == bricks[:, None]).astype(jnp.float32)
        highest = lax.Precision.HIGHEST
        placed_weighted = jnp.einsum("bs,sij->bij", place, slot_weighted, precision=highest)
        placed_weights = jnp.einsum("bs,sij->bij", place, slot_weights, precision=highest)
        if weighted is None:
            weighted, weights = placed_weighted, placed_weights
        else:
            weighted, weights = weighted + placed_weighted, weights + placed_weights
    if n_view == 2:
        numer, denom = swap_halves(weighted), swap_halves(weights)
    else:
        numer, denom = (
            lax.psum_scatter(weighted, "view", scatter_dimension=1, tiled=True),
            lax.psum_scatter(weights, "view", scatter_dimension=1, tiled=True),
        )
    return numer / jnp.maximum(denom, 1.0)


def solution(mesh):
    placed = (
        P("view", "brick", None),
        P(None, "view", "brick"),
        P("view", "brick", None, None),
        P("view", "brick"),
    )
    return jax.shard_map(
        functools.partial(local, mesh.shape["view"]), mesh=mesh, in_specs=placed, out_specs=P("brick", "view", None), check_vma=False
    )
```

```python
import functools

import jax
import jax.numpy as jnp
from jax import lax
from jax.sharding import PartitionSpec as P

BS = 128
BLUR = 4
SMOOTH = 4
BRICKS_DEV = 28
WIN = 144
EDGE = 160
LANES = 128
RING_GROUP = 4


def blur_matrix(out_len, radius):
    out_index = jnp.arange(out_len)[:, None]
    in_index = jnp.arange(out_len + 2 * radius)[None, :]
    offset = (in_index - out_index - radius).astype(jnp.float32)
    spread_px = radius / 2.0
    tap_values = jnp.exp(-offset * offset / (2.0 * spread_px * spread_px))
    tap_line = jnp.arange(-radius, radius + 1).astype(jnp.float32)
    tap_sum = jnp.sum(jnp.exp(-tap_line * tap_line / (2.0 * spread_px * spread_px)))
    inside = jnp.abs(offset) <= radius
    return jnp.where(inside, tap_values / tap_sum, jnp.zeros_like(tap_values))


def contrast(windows):
    inner_len = WIN - 2 * BLUR
    highest = lax.Precision.HIGH
    first_blur = blur_matrix(inner_len, BLUR)
    second_blur = blur_matrix(BS, SMOOTH)
    row_pass = jnp.einsum("ow,nwv->nov", first_blur, windows, precision=highest)
    local_mean = jnp.einsum("nov,pv->nop", row_pass, first_blur, precision=highest)
    inner_part = windows[:, BLUR : BLUR + inner_len, BLUR : BLUR + inner_len]
    energy = (inner_part - local_mean) ** 2
    row_two = jnp.einsum("ow,nwv->nov", second_blur, energy, precision=highest)
    weight = jnp.einsum("nov,pv->nop", row_two, second_blur, precision=highest)
    margin = BLUR + SMOOTH
    center = windows[:, margin : margin + BS, margin : margin + BS]
    return (weight * center, weight)


def cut_windows(square, shift_row, shift_col):
    highest = lax.Precision.HIGHEST
    span = jnp.arange(WIN)[None, :, None]
    cells = jnp.arange(EDGE)[None, None, :]
    pick_rows = (span + shift_row[:, None, None] == cells).astype(jnp.float32)
    pick_cols = (span + shift_col[:, None, None] == cells).astype(jnp.float32)
    rows_cut = jnp.einsum("nie,nef->nif", pick_rows, square, precision=highest)
    return jnp.einsum("nif,njf->nij", rows_cut, pick_cols, precision=highest)


def arrange_slots(arrived, labels):
    flat_slots = arrived.reshape((-1,) + arrived.shape[2:])
    label_ids = labels.reshape(-1).astype(jnp.int32)
    matches = (label_ids[:, None] == jnp.arange(BRICKS_DEV)[None, :]).astype(jnp.int32)
    slot_of = jnp.argmax(matches, axis=0)
    present = jnp.max(matches, axis=0).astype(jnp.float32)
    return flat_slots[slot_of] * present[:, None, None]


def swap_halves(part):
    me = lax.axis_index("view")
    halves = part.reshape(part.shape[0], 2, part.shape[1] // 2, part.shape[2])
    kept = lax.dynamic_index_in_dim(halves, me, axis=1, keepdims=False)
    outgoing = lax.dynamic_index_in_dim(halves, 1 - me, axis=1, keepdims=False)
    arrived = lax.ppermute(outgoing, "view", perm=[(0, 1), (1, 0)])
    return kept + arrived


def local(n_view, tiles, shifts, footprint, target):
    count = tiles.shape[1]
    flat = lax.optimization_barrier(tiles.reshape(count, EDGE * EDGE // LANES, LANES))
    square = flat.reshape(count, EDGE, EDGE)
    windows = cut_windows(square, shifts[0, 0], shifts[1, 0])
    slot_list = footprint[0, 0]
    filled = slot_list >= 0
    picked = jnp.maximum(slot_list, 0)
    labels = jnp.where(filled, target[0][picked], -1).astype(jnp.float32)
    owners, cap = slot_list.shape
    dense_rows = WIN * WIN // LANES
    bricks = jnp.arange(BRICKS_DEV)
    mask = filled.astype(jnp.float32)[:, :, None, None]
    packed = (windows[picked] * mask).reshape(owners, cap, dense_rows, LANES)
    label_row = jnp.broadcast_to(labels[:, :, None, None], (owners, cap, 1, LANES))
    payload = jnp.concatenate([packed, label_row], axis=2)
    me = lax.axis_index("brick")
    weighted = weights = None
    previous = None
    for first in range(0, owners, RING_GROUP):
        shifts_here = list(range(first, min(first + RING_GROUP, owners)))
        blocks = [
            lax.dynamic_index_in_dim(payload, (me + shift) % owners, axis=0, keepdims=False)
            for shift in shifts_here
        ]
        if previous is not None:
            blocks, _ = lax.optimization_barrier((blocks, previous))
        arrivals = []
        for shift, block in zip(shifts_here, blocks):
            if shift:
                ring = [(src, (src + shift) % owners) for src in range(owners)]
                block = lax.ppermute(block, "brick", perm=ring)
            arrivals.append(block)
        if weighted is not None:
            weighted, weights, arrivals = lax.optimization_barrier((weighted, weights, arrivals))
        previous = arrivals
        arrived = jnp.stack(arrivals).reshape(len(arrivals) * cap, dense_rows + 1, LANES)
        arrived_labels = arrived[:, dense_rows, 0].astype(jnp.int32)
        slots = arrived[:, :dense_rows].reshape(len(arrivals) * cap, WIN, WIN)
        slot_weighted, slot_weights = contrast(slots)
        place = (arrived_labels[None, :] == bricks[:, None]).astype(jnp.float32)
        highest = lax.Precision.HIGHEST
        placed_weighted = jnp.einsum("bs,sij->bij", place, slot_weighted, precision=highest)
        placed_weights = jnp.einsum("bs,sij->bij", place, slot_weights, precision=highest)
        if weighted is None:
            weighted, weights = placed_weighted, placed_weights
        else:
            weighted, weights = weighted + placed_weighted, weights + placed_weights
    if n_view == 2:
        numer, denom = swap_halves(weighted), swap_halves(weights)
    else:
        numer, denom = (
            lax.psum_scatter(weighted, "view", scatter_dimension=1, tiled=True),
            lax.psum_scatter(weights, "view", scatter_dimension=1, tiled=True),
        )
    return numer / jnp.maximum(denom, 1.0)


def solution(mesh):
    placed = (
        P("view", "brick", None),
        P(None, "view", "brick"),
        P("view", "brick", None, None),
        P("view", "brick"),
    )
    return jax.shard_map(
        functools.partial(local, mesh.shape["view"]), mesh=mesh, in_specs=placed, out_specs=P("brick", "view", None), check_vma=False
    )
```

```python
import functools

import jax
import jax.numpy as jnp
from jax import lax
from jax.sharding import PartitionSpec as P

BS = 128
BLUR = 4
SMOOTH = 4
BRICKS_DEV = 28
WIN = 144
EDGE = 160
LANES = 128


def blur_matrix(out_len, radius):
    out_index = jnp.arange(out_len)[:, None]
    in_index = jnp.arange(out_len + 2 * radius)[None, :]
    offset = (in_index - out_index - radius).astype(jnp.float32)
    spread_px = radius / 2.0
    tap_values = jnp.exp(-offset * offset / (2.0 * spread_px * spread_px))
    tap_line = jnp.arange(-radius, radius + 1).astype(jnp.float32)
    tap_sum = jnp.sum(jnp.exp(-tap_line * tap_line / (2.0 * spread_px * spread_px)))
    inside = jnp.abs(offset) <= radius
    return jnp.where(inside, tap_values / tap_sum, jnp.zeros_like(tap_values))


def contrast(windows):
    inner_len = WIN - 2 * BLUR
    highest = lax.Precision.HIGH
    first_blur = blur_matrix(inner_len, BLUR)
    second_blur = blur_matrix(BS, SMOOTH)
    row_pass = jnp.einsum("ow,nwv->nov", first_blur, windows, precision=highest)
    local_mean = jnp.einsum("nov,pv->nop", row_pass, first_blur, precision=highest)
    inner_part = windows[:, BLUR : BLUR + inner_len, BLUR : BLUR + inner_len]
    energy = (inner_part - local_mean) ** 2
    row_two = jnp.einsum("ow,nwv->nov", second_blur, energy, precision=highest)
    weight = jnp.einsum("nov,pv->nop", row_two, second_blur, precision=highest)
    margin = BLUR + SMOOTH
    center = windows[:, margin : margin + BS, margin : margin + BS]
    return (weight * center, weight)


def cut_windows(square, shift_row, shift_col):
    highest = lax.Precision.HIGHEST
    span = jnp.arange(WIN)[None, :, None]
    cells = jnp.arange(EDGE)[None, None, :]
    pick_rows = (span + shift_row[:, None, None] == cells).astype(jnp.float32)
    pick_cols = (span + shift_col[:, None, None] == cells).astype(jnp.float32)
    rows_cut = jnp.einsum("nie,nef->nif", pick_rows, square, precision=highest)
    return jnp.einsum("nif,njf->nij", rows_cut, pick_cols, precision=highest)


def arrange_slots(arrived, labels):
    flat_slots = arrived.reshape((-1,) + arrived.shape[2:])
    label_ids = labels.reshape(-1).astype(jnp.int32)
    matches = (label_ids[:, None] == jnp.arange(BRICKS_DEV)[None, :]).astype(jnp.int32)
    slot_of = jnp.argmax(matches, axis=0)
    present = jnp.max(matches, axis=0).astype(jnp.float32)
    return flat_slots[slot_of] * present[:, None, None]


def swap_halves(part):
    me = lax.axis_index("view")
    halves = part.reshape(part.shape[0], 2, part.shape[1] // 2, part.shape[2])
    kept = lax.dynamic_index_in_dim(halves, me, axis=1, keepdims=False)
    outgoing = lax.dynamic_index_in_dim(halves, 1 - me, axis=1, keepdims=False)
    arrived = lax.ppermute(outgoing, "view", perm=[(0, 1), (1, 0)])
    return kept + arrived


def local(n_view, tiles, shifts, footprint, target):
    count = tiles.shape[1]
    flat = lax.optimization_barrier(tiles.reshape(count, EDGE * EDGE // LANES, LANES))
    square = flat.reshape(count, EDGE, EDGE)
    windows = cut_windows(square, shifts[0, 0], shifts[1, 0])
    slot_list = footprint[0, 0]
    filled = slot_list >= 0
    picked = jnp.maximum(slot_list, 0)
    labels = jnp.where(filled, target[0][picked], -1).astype(jnp.float32)
    owners, cap = slot_list.shape
    dense_rows = WIN * WIN // LANES
    bricks = jnp.arange(BRICKS_DEV)
    dense_windows = windows.reshape(windows.shape[0], dense_rows, LANES)
    weighted = weights = None
    for slot in range(cap):
        mask = filled[:, slot].astype(jnp.float32)[:, None, None]
        packed = dense_windows[picked[:, slot]] * mask
        label_row = jnp.broadcast_to(labels[:, slot, None, None], (owners, 1, LANES))
        payload = jnp.concatenate([packed, label_row], axis=1)
        arrived = lax.all_to_all(payload, "brick", split_axis=0, concat_axis=0, tiled=True)
        arrived_labels = arrived[:, dense_rows, 0].astype(jnp.int32)
        slots = arrived[:, :dense_rows].reshape(owners, WIN, WIN)
        slot_weighted, slot_weights = contrast(slots)
        place = (arrived_labels[None, :] == bricks[:, None]).astype(jnp.float32)
        highest = lax.Precision.HIGHEST
        placed_weighted = jnp.einsum("bs,sij->bij", place, slot_weighted, precision=highest)
        placed_weights = jnp.einsum("bs,sij->bij", place, slot_weights, precision=highest)
        if weighted is None:
            weighted, weights = placed_weighted, placed_weights
        else:
            weighted, weights = weighted + placed_weighted, weights + placed_weights
    if n_view == 2:
        numer, denom = swap_halves(weighted), swap_halves(weights)
    else:
        numer, denom = (
            lax.psum_scatter(weighted, "view", scatter_dimension=1, tiled=True),
            lax.psum_scatter(weights, "view", scatter_dimension=1, tiled=True),
        )
    return numer / jnp.maximum(denom, 1.0)


def solution(mesh):
    placed = (
        P("view", "brick", None),
        P(None, "view", "brick"),
        P("view", "brick", None, None),
        P("view", "brick"),
    )
    return jax.shard_map(
        functools.partial(local, mesh.shape["view"]), mesh=mesh, in_specs=placed, out_specs=P("brick", "view", None), check_vma=False
    )
```

```python
import functools

import jax
import jax.numpy as jnp
from jax import lax
from jax.sharding import PartitionSpec as P

BS = 128
BLUR = 4
SMOOTH = 4
BRICKS_DEV = 28
WIN = 144
EDGE = 160
LANES = 128


def blur_matrix(out_len, radius):
    out_index = jnp.arange(out_len)[:, None]
    in_index = jnp.arange(out_len + 2 * radius)[None, :]
    offset = (in_index - out_index - radius).astype(jnp.float32)
    spread_px = radius / 2.0
    tap_values = jnp.exp(-offset * offset / (2.0 * spread_px * spread_px))
    tap_line = jnp.arange(-radius, radius + 1).astype(jnp.float32)
    tap_sum = jnp.sum(jnp.exp(-tap_line * tap_line / (2.0 * spread_px * spread_px)))
    inside = jnp.abs(offset) <= radius
    return jnp.where(inside, tap_values / tap_sum, jnp.zeros_like(tap_values))


def contrast(windows):
    inner_len = WIN - 2 * BLUR
    highest = lax.Precision.HIGH
    first_blur = blur_matrix(inner_len, BLUR)
    second_blur = blur_matrix(BS, SMOOTH)
    row_pass = jnp.einsum("ow,nwv->nov", first_blur, windows, precision=highest)
    local_mean = jnp.einsum("nov,pv->nop", row_pass, first_blur, precision=highest)
    inner_part = windows[:, BLUR : BLUR + inner_len, BLUR : BLUR + inner_len]
    energy = (inner_part - local_mean) ** 2
    row_two = jnp.einsum("ow,nwv->nov", second_blur, energy, precision=highest)
    weight = jnp.einsum("nov,pv->nop", row_two, second_blur, precision=highest)
    margin = BLUR + SMOOTH
    center = windows[:, margin : margin + BS, margin : margin + BS]
    return (weight * center, weight)


def cut_windows(square, shift_row, shift_col):
    highest = lax.Precision.HIGH
    span = jnp.arange(WIN)[None, :, None]
    cells = jnp.arange(EDGE)[None, None, :]
    pick_rows = (span + shift_row[:, None, None] == cells).astype(jnp.float32)
    pick_cols = (span + shift_col[:, None, None] == cells).astype(jnp.float32)
    rows_cut = jnp.einsum("nie,nef->nif", pick_rows, square, precision=highest)
    return jnp.einsum("nif,njf->nij", rows_cut, pick_cols, precision=highest)


def arrange_slots(arrived, labels):
    flat_slots = arrived.reshape((-1,) + arrived.shape[2:])
    label_ids = labels.reshape(-1).astype(jnp.int32)
    matches = (label_ids[:, None] == jnp.arange(BRICKS_DEV)[None, :]).astype(jnp.int32)
    slot_of = jnp.argmax(matches, axis=0)
    present = jnp.max(matches, axis=0).astype(jnp.float32)
    return flat_slots[slot_of] * present[:, None, None]


def swap_halves(part):
    me = lax.axis_index("view")
    halves = part.reshape(part.shape[0], 2, part.shape[1] // 2, part.shape[2])
    kept = lax.dynamic_index_in_dim(halves, me, axis=1, keepdims=False)
    outgoing = lax.dynamic_index_in_dim(halves, 1 - me, axis=1, keepdims=False)
    arrived = lax.ppermute(outgoing, "view", perm=[(0, 1), (1, 0)])
    return kept + arrived


def local(n_view, tiles, shifts, footprint, target):
    count = tiles.shape[1]
    flat = lax.optimization_barrier(tiles.reshape(count, EDGE * EDGE // LANES, LANES))
    square = flat.reshape(count, EDGE, EDGE)
    windows = cut_windows(square, shifts[0, 0], shifts[1, 0])
    slot_list = footprint[0, 0]
    filled = slot_list >= 0
    picked = jnp.maximum(slot_list, 0)
    labels = jnp.where(filled, target[0][picked], -1).astype(jnp.float32)
    owners, cap = slot_list.shape
    dense_rows = WIN * WIN // LANES
    bricks = jnp.arange(BRICKS_DEV)
    dense_windows = windows.reshape(windows.shape[0], dense_rows, LANES)
    weighted = weights = None
    for slot in range(cap):
        mask = filled[:, slot].astype(jnp.float32)[:, None, None]
        packed = dense_windows[picked[:, slot]] * mask
        label_row = jnp.broadcast_to(labels[:, slot, None, None], (owners, 1, LANES))
        payload = jnp.concatenate([packed, label_row], axis=1)
        arrived = lax.all_to_all(payload, "brick", split_axis=0, concat_axis=0, tiled=True)
        arrived_labels = arrived[:, dense_rows, 0].astype(jnp.int32)
        slots = arrived[:, :dense_rows].reshape(owners, WIN, WIN)
        slot_weighted, slot_weights = contrast(slots)
        place = (arrived_labels[None, :] == bricks[:, None]).astype(jnp.float32)
        highest = lax.Precision.HIGH
        placed_weighted = jnp.einsum("bs,sij->bij", place, slot_weighted, precision=highest)
        placed_weights = jnp.einsum("bs,sij->bij", place, slot_weights, precision=highest)
        if weighted is None:
            weighted, weights = placed_weighted, placed_weights
        else:
            weighted, weights = weighted + placed_weighted, weights + placed_weights
    if n_view == 2:
        numer, denom = swap_halves(weighted), swap_halves(weights)
    else:
        numer, denom = (
            lax.psum_scatter(weighted, "view", scatter_dimension=1, tiled=True),
            lax.psum_scatter(weights, "view", scatter_dimension=1, tiled=True),
        )
    return numer / jnp.maximum(denom, 1.0)


def solution(mesh):
    placed = (
        P("view", "brick", None),
        P(None, "view", "brick"),
        P("view", "brick", None, None),
        P("view", "brick"),
    )
    return jax.shard_map(
        functools.partial(local, mesh.shape["view"]), mesh=mesh, in_specs=placed, out_specs=P("brick", "view", None), check_vma=False
    )
```

```python
import functools

import jax
import jax.numpy as jnp
from jax import lax
from jax.sharding import PartitionSpec as P

BS = 128
BLUR = 4
SMOOTH = 4
BRICKS_DEV = 28
WIN = 144
EDGE = 160
LANES = 128


def blur_matrix(out_len, radius):
    out_index = jnp.arange(out_len)[:, None]
    in_index = jnp.arange(out_len + 2 * radius)[None, :]
    offset = (in_index - out_index - radius).astype(jnp.float32)
    spread_px = radius / 2.0
    tap_values = jnp.exp(-offset * offset / (2.0 * spread_px * spread_px))
    tap_line = jnp.arange(-radius, radius + 1).astype(jnp.float32)
    tap_sum = jnp.sum(jnp.exp(-tap_line * tap_line / (2.0 * spread_px * spread_px)))
    inside = jnp.abs(offset) <= radius
    return jnp.where(inside, tap_values / tap_sum, jnp.zeros_like(tap_values))


def contrast(slab):
    highest = lax.Precision.HIGH
    rows = slab.shape[1]
    inner_rows = rows - 2 * BLUR
    out_rows = inner_rows - 2 * SMOOTH
    inner_len = WIN - 2 * BLUR
    first_rows = blur_matrix(inner_rows, BLUR)
    first_cols = blur_matrix(inner_len, BLUR)
    second_rows = blur_matrix(out_rows, SMOOTH)
    second_cols = blur_matrix(BS, SMOOTH)
    row_pass = jnp.einsum("ow,nwv->nov", first_rows, slab, precision=highest)
    local_mean = jnp.einsum("nov,pv->nop", row_pass, first_cols, precision=highest)
    inner_part = slab[:, BLUR : BLUR + inner_rows, BLUR : BLUR + inner_len]
    energy = (inner_part - local_mean) ** 2
    row_two = jnp.einsum("ow,nwv->nov", second_rows, energy, precision=highest)
    weight = jnp.einsum("nov,pv->nop", row_two, second_cols, precision=highest)
    margin = BLUR + SMOOTH
    center = slab[:, margin : margin + out_rows, margin : margin + BS]
    return (weight * center, weight)


def cut_windows(square, shift_row, shift_col):
    highest = lax.Precision.HIGH
    span = jnp.arange(WIN)[None, :, None]
    cells = jnp.arange(EDGE)[None, None, :]
    pick_rows = (span + shift_row[:, None, None] == cells).astype(jnp.float32)
    pick_cols = (span + shift_col[:, None, None] == cells).astype(jnp.float32)
    rows_cut = jnp.einsum("nie,nef->nif", pick_rows, square, precision=highest)
    return jnp.einsum("nif,njf->nij", rows_cut, pick_cols, precision=highest)


def arrange_slots(arrived, labels):
    flat_slots = arrived.reshape((-1,) + arrived.shape[2:])
    label_ids = labels.reshape(-1).astype(jnp.int32)
    matches = (label_ids[:, None] == jnp.arange(BRICKS_DEV)[None, :]).astype(jnp.int32)
    slot_of = jnp.argmax(matches, axis=0)
    present = jnp.max(matches, axis=0).astype(jnp.float32)
    return flat_slots[slot_of] * present[:, None, None]


def swap_halves(part):
    me = lax.axis_index("view")
    halves = part.reshape(part.shape[0], 2, part.shape[1] // 2, part.shape[2])
    kept = lax.dynamic_index_in_dim(halves, me, axis=1, keepdims=False)
    outgoing = lax.dynamic_index_in_dim(halves, 1 - me, axis=1, keepdims=False)
    arrived = lax.ppermute(outgoing, "view", perm=[(0, 1), (1, 0)])
    return kept + arrived


def swap_pair(top, bottom):
    me = lax.axis_index("view")
    halves = jnp.stack([top, bottom], axis=1)
    kept = lax.dynamic_index_in_dim(halves, me, axis=1, keepdims=False)
    outgoing = lax.dynamic_index_in_dim(halves, 1 - me, axis=1, keepdims=False)
    arrived = lax.ppermute(outgoing, "view", perm=[(0, 1), (1, 0)])
    return kept + arrived


def local(n_view, tiles, shifts, footprint, target):
    count = tiles.shape[1]
    flat = lax.optimization_barrier(tiles.reshape(count, EDGE * EDGE // LANES, LANES))
    square = flat.reshape(count, EDGE, EDGE)
    windows = cut_windows(square, shifts[0, 0], shifts[1, 0])
    slot_list = footprint[0, 0]
    filled = slot_list >= 0
    picked = jnp.maximum(slot_list, 0)
    labels = jnp.where(filled, target[0][picked], -1).astype(jnp.float32)
    owners, cap = slot_list.shape
    dense_rows = WIN * WIN // LANES
    bricks = jnp.arange(BRICKS_DEV)
    dense_windows = windows.reshape(windows.shape[0], dense_rows, LANES)
    highest = lax.Precision.HIGH
    half = BS // 2
    slab_rows = half + 2 * (BLUR + SMOOTH)
    head_rows = slab_rows * WIN // LANES
    masks = filled.astype(jnp.float32)[:, :, None, None]
    first = dense_windows[picked[:, 0]] * masks[:, 0]
    second = dense_windows[picked[:, 1]] * masks[:, 1]
    label_rows = jnp.broadcast_to(labels[:, :, None], (owners, cap, LANES))
    payload = jnp.concatenate([first, second[:, :head_rows], label_rows], axis=1)
    arrived = lax.all_to_all(payload, "brick", split_axis=0, concat_axis=0, tiled=True)
    late = lax.all_to_all(second[:, head_rows:], "brick", split_axis=0, concat_axis=0, tiled=True)
    label_at = dense_rows + head_rows
    first_labels = arrived[:, label_at, 0].astype(jnp.int32)
    second_labels = arrived[:, label_at + 1, 0].astype(jnp.int32)
    first_place = (first_labels[None, :] == bricks[:, None]).astype(jnp.float32)
    second_place = (second_labels[None, :] == bricks[:, None]).astype(jnp.float32)
    first_weighted, first_weights = contrast(arrived[:, :dense_rows].reshape(owners, WIN, WIN))
    upper = arrived[:, dense_rows:label_at].reshape(owners, slab_rows, WIN)
    upper_weighted, upper_weights = contrast(upper)
    top_n = jnp.einsum("bs,sij->bij", first_place, first_weighted[:, :half], precision=highest)
    top_n = top_n + jnp.einsum("bs,sij->bij", second_place, upper_weighted, precision=highest)
    top_d = jnp.einsum("bs,sij->bij", first_place, first_weights[:, :half], precision=highest)
    top_d = top_d + jnp.einsum("bs,sij->bij", second_place, upper_weights, precision=highest)
    bottom_n = jnp.einsum("bs,sij->bij", first_place, first_weighted[:, half:], precision=highest)
    bottom_d = jnp.einsum("bs,sij->bij", first_place, first_weights[:, half:], precision=highest)
    top_n, top_d, bottom_n, bottom_d, late = lax.optimization_barrier((top_n, top_d, bottom_n, bottom_d, late))
    lower = jnp.concatenate([upper[:, half:], late.reshape(owners, WIN - slab_rows, WIN)], axis=1)
    lower_weighted, lower_weights = contrast(lower)
    bottom_n = bottom_n + jnp.einsum("bs,sij->bij", second_place, lower_weighted, precision=highest)
    bottom_d = bottom_d + jnp.einsum("bs,sij->bij", second_place, lower_weights, precision=highest)
    if n_view == 2:
        numer, denom = swap_pair(top_n, bottom_n), swap_pair(top_d, bottom_d)
    else:
        numer, denom = (
            lax.psum_scatter(jnp.concatenate([top_n, bottom_n], axis=1), "view", scatter_dimension=1, tiled=True),
            lax.psum_scatter(jnp.concatenate([top_d, bottom_d], axis=1), "view", scatter_dimension=1, tiled=True),
        )
    return numer / jnp.maximum(denom, 1.0)


def solution(mesh):
    placed = (
        P("view", "brick", None),
        P(None, "view", "brick"),
        P("view", "brick", None, None),
        P("view", "brick"),
    )
    return jax.shard_map(
        functools.partial(local, mesh.shape["view"]), mesh=mesh, in_specs=placed, out_specs=P("brick", "view", None), check_vma=False
    )
```

```python
import functools

import jax
import jax.numpy as jnp
from jax import lax
from jax.sharding import PartitionSpec as P

BS = 128
BLUR = 4
SMOOTH = 4
BRICKS_DEV = 28
WIN = 144
EDGE = 160
LANES = 128


def blur_matrix(out_len, radius):
    out_index = jnp.arange(out_len)[:, None]
    in_index = jnp.arange(out_len + 2 * radius)[None, :]
    offset = (in_index - out_index - radius).astype(jnp.float32)
    spread_px = radius / 2.0
    tap_values = jnp.exp(-offset * offset / (2.0 * spread_px * spread_px))
    tap_line = jnp.arange(-radius, radius + 1).astype(jnp.float32)
    tap_sum = jnp.sum(jnp.exp(-tap_line * tap_line / (2.0 * spread_px * spread_px)))
    inside = jnp.abs(offset) <= radius
    return jnp.where(inside, tap_values / tap_sum, jnp.zeros_like(tap_values))


def contrast(windows):
    inner_len = WIN - 2 * BLUR
    highest = lax.Precision.HIGH
    first_blur = blur_matrix(inner_len, BLUR)
    second_blur = blur_matrix(BS, SMOOTH)
    row_pass = jnp.einsum("ow,nwv->nov", first_blur, windows, precision=highest)
    local_mean = jnp.einsum("nov,pv->nop", row_pass, first_blur, precision=highest)
    inner_part = windows[:, BLUR : BLUR + inner_len, BLUR : BLUR + inner_len]
    energy = (inner_part - local_mean) ** 2
    row_two = jnp.einsum("ow,nwv->nov", second_blur, energy, precision=highest)
    weight = jnp.einsum("nov,pv->nop", row_two, second_blur, precision=highest)
    margin = BLUR + SMOOTH
    center = windows[:, margin : margin + BS, margin : margin + BS]
    return (weight * center, weight)


def cut_windows(square, shift_row, shift_col):
    highest = lax.Precision.HIGH
    span = jnp.arange(WIN)[None, :, None]
    cells = jnp.arange(EDGE)[None, None, :]
    pick_rows = (span + shift_row[:, None, None] == cells).astype(jnp.float32)
    pick_cols = (span + shift_col[:, None, None] == cells).astype(jnp.float32)
    rows_cut = jnp.einsum("nie,nef->nif", pick_rows, square, precision=highest)
    return jnp.einsum("nif,njf->nij", rows_cut, pick_cols, precision=highest)


def arrange_slots(arrived, labels):
    flat_slots = arrived.reshape((-1,) + arrived.shape[2:])
    label_ids = labels.reshape(-1).astype(jnp.int32)
    matches = (label_ids[:, None] == jnp.arange(BRICKS_DEV)[None, :]).astype(jnp.int32)
    slot_of = jnp.argmax(matches, axis=0)
    present = jnp.max(matches, axis=0).astype(jnp.float32)
    return flat_slots[slot_of] * present[:, None, None]


def swap_halves(part):
    me = lax.axis_index("view")
    halves = part.reshape(part.shape[0], 2, part.shape[1] // 2, part.shape[2])
    kept = lax.dynamic_index_in_dim(halves, me, axis=1, keepdims=False)
    outgoing = lax.dynamic_index_in_dim(halves, 1 - me, axis=1, keepdims=False)
    arrived = lax.ppermute(outgoing, "view", perm=[(0, 1), (1, 0)])
    return kept + arrived


def local(n_view, tiles, shifts, footprint, target):
    count = tiles.shape[1]
    flat = lax.optimization_barrier(tiles.reshape(count, EDGE * EDGE // LANES, LANES))
    square = flat.reshape(count, EDGE, EDGE)
    windows = cut_windows(square, shifts[0, 0], shifts[1, 0])
    slot_list = footprint[0, 0]
    filled = slot_list >= 0
    picked = jnp.maximum(slot_list, 0)
    labels = jnp.where(filled, target[0][picked], -1).astype(jnp.float32)
    owners, cap = slot_list.shape
    dense_rows = WIN * WIN // LANES
    bricks = jnp.arange(BRICKS_DEV)
    dense_windows = windows.reshape(windows.shape[0], dense_rows, LANES)
    weighted = weights = None
    for slot in range(cap):
        mask = filled[:, slot].astype(jnp.float32)[:, None, None]
        packed = dense_windows[picked[:, slot]] * mask
        label_row = jnp.broadcast_to(labels[:, slot, None, None], (owners, 1, LANES))
        payload = jnp.concatenate([packed, label_row], axis=1)
        arrived = lax.all_to_all(payload, "brick", split_axis=0, concat_axis=0, tiled=True)
        arrived_labels = arrived[:, dense_rows, 0].astype(jnp.int32)
        slots = arrived[:, :dense_rows].reshape(owners, WIN, WIN)
        slot_weighted, slot_weights = contrast(slots)
        place = (arrived_labels[None, :] == bricks[:, None]).astype(jnp.float32)
        highest = lax.Precision.HIGH
        if n_view == 2 and slot == cap - 1:
            me = lax.axis_index("view")
            pair = [(0, 1), (1, 0)]
            other_labels = lax.ppermute(arrived[:, dense_rows, 0], "view", perm=pair).astype(jnp.int32)
            other_place = (other_labels[None, :] == bricks[:, None]).astype(jnp.float32)
            sums = []
            for part in (slot_weighted, slot_weights):
                halves = part.reshape(owners, 2, BS // 2, BS)
                kept = lax.dynamic_index_in_dim(halves, me, axis=1, keepdims=False)
                outgoing = lax.dynamic_index_in_dim(halves, 1 - me, axis=1, keepdims=False)
                received = lax.ppermute(outgoing, "view", perm=pair)
                own = jnp.einsum("bs,sij->bij", place, kept, precision=highest)
                sums.append(own + jnp.einsum("bs,sij->bij", other_place, received, precision=highest))
            placed_weighted, placed_weights = sums
        else:
            placed_weighted = jnp.einsum("bs,sij->bij", place, slot_weighted, precision=highest)
            placed_weights = jnp.einsum("bs,sij->bij", place, slot_weights, precision=highest)
            if n_view == 2:
                placed_weighted = swap_halves(placed_weighted)
                placed_weights = swap_halves(placed_weights)
        if weighted is None:
            weighted, weights = placed_weighted, placed_weights
        else:
            weighted, weights = weighted + placed_weighted, weights + placed_weights
    if n_view == 2:
        numer, denom = weighted, weights
    else:
        numer, denom = (
            lax.psum_scatter(weighted, "view", scatter_dimension=1, tiled=True),
            lax.psum_scatter(weights, "view", scatter_dimension=1, tiled=True),
        )
    return numer / jnp.maximum(denom, 1.0)


def solution(mesh):
    placed = (
        P("view", "brick", None),
        P(None, "view", "brick"),
        P("view", "brick", None, None),
        P("view", "brick"),
    )
    return jax.shard_map(
        functools.partial(local, mesh.shape["view"]), mesh=mesh, in_specs=placed, out_specs=P("brick", "view", None), check_vma=False
    )
```

```python
import functools

import jax
import jax.numpy as jnp
from jax import lax
from jax.sharding import PartitionSpec as P

BS = 128
BLUR = 4
SMOOTH = 4
BRICKS_DEV = 28
WIN = 144
EDGE = 160
LANES = 128


def blur_matrix(out_len, radius):
    out_index = jnp.arange(out_len)[:, None]
    in_index = jnp.arange(out_len + 2 * radius)[None, :]
    offset = (in_index - out_index - radius).astype(jnp.float32)
    spread_px = radius / 2.0
    tap_values = jnp.exp(-offset * offset / (2.0 * spread_px * spread_px))
    tap_line = jnp.arange(-radius, radius + 1).astype(jnp.float32)
    tap_sum = jnp.sum(jnp.exp(-tap_line * tap_line / (2.0 * spread_px * spread_px)))
    inside = jnp.abs(offset) <= radius
    return jnp.where(inside, tap_values / tap_sum, jnp.zeros_like(tap_values))


def contrast(windows):
    inner_len = WIN - 2 * BLUR
    exact = lax.Precision.HIGHEST
    highest = lax.Precision.HIGH
    first_blur = blur_matrix(inner_len, BLUR)
    second_blur = blur_matrix(BS, SMOOTH)
    row_pass = jnp.einsum("ow,nwv->nov", first_blur, windows, precision=exact)
    local_mean = jnp.einsum("nov,pv->nop", row_pass, first_blur, precision=exact)
    inner_part = windows[:, BLUR : BLUR + inner_len, BLUR : BLUR + inner_len]
    energy = (inner_part - local_mean) ** 2
    row_two = jnp.einsum("ow,nwv->nov", second_blur, energy, precision=highest)
    weight = jnp.einsum("nov,pv->nop", row_two, second_blur, precision=highest)
    margin = BLUR + SMOOTH
    center = windows[:, margin : margin + BS, margin : margin + BS]
    return (weight * center, weight)


def cut_windows(square, shift_row, shift_col):
    highest = lax.Precision.HIGHEST
    span = jnp.arange(WIN)[None, :, None]
    cells = jnp.arange(EDGE)[None, None, :]
    pick_rows = (span + shift_row[:, None, None] == cells).astype(jnp.float32)
    pick_cols = (span + shift_col[:, None, None] == cells).astype(jnp.float32)
    rows_cut = jnp.einsum("nie,nef->nif", pick_rows, square, precision=highest)
    return jnp.einsum("nif,njf->nij", rows_cut, pick_cols, precision=highest)


def arrange_slots(arrived, labels):
    flat_slots = arrived.reshape((-1,) + arrived.shape[2:])
    label_ids = labels.reshape(-1).astype(jnp.int32)
    matches = (label_ids[:, None] == jnp.arange(BRICKS_DEV)[None, :]).astype(jnp.int32)
    slot_of = jnp.argmax(matches, axis=0)
    present = jnp.max(matches, axis=0).astype(jnp.float32)
    return flat_slots[slot_of] * present[:, None, None]


def swap_halves(part):
    me = lax.axis_index("view")
    halves = part.reshape(part.shape[0], 2, part.shape[1] // 2, part.shape[2])
    kept = lax.dynamic_index_in_dim(halves, me, axis=1, keepdims=False)
    outgoing = lax.dynamic_index_in_dim(halves, 1 - me, axis=1, keepdims=False)
    arrived = lax.ppermute(outgoing, "view", perm=[(0, 1), (1, 0)])
    return kept + arrived


def local(n_view, tiles, shifts, footprint, target):
    count = tiles.shape[1]
    flat = lax.optimization_barrier(tiles.reshape(count, EDGE * EDGE // LANES, LANES))
    square = flat.reshape(count, EDGE, EDGE)
    windows = cut_windows(square, shifts[0, 0], shifts[1, 0])
    slot_list = footprint[0, 0]
    filled = slot_list >= 0
    picked = jnp.maximum(slot_list, 0)
    labels = jnp.where(filled, target[0][picked], -1).astype(jnp.float32)
    owners, cap = slot_list.shape
    dense_rows = WIN * WIN // LANES
    bricks = jnp.arange(BRICKS_DEV)
    dense_windows = windows.reshape(windows.shape[0], dense_rows, LANES)
    weighted = weights = None
    for slot in range(cap):
        mask = filled[:, slot].astype(jnp.float32)[:, None, None]
        packed = dense_windows[picked[:, slot]] * mask
        label_row = jnp.broadcast_to(labels[:, slot, None, None], (owners, 1, LANES))
        payload = jnp.concatenate([packed, label_row], axis=1)
        arrived = lax.all_to_all(payload, "brick", split_axis=0, concat_axis=0, tiled=True)
        arrived_labels = arrived[:, dense_rows, 0].astype(jnp.int32)
        slots = arrived[:, :dense_rows].reshape(owners, WIN, WIN)
        slot_weighted, slot_weights = contrast(slots)
        place = (arrived_labels[None, :] == bricks[:, None]).astype(jnp.float32)
        highest = lax.Precision.HIGH
        placed_weighted = jnp.einsum("bs,sij->bij", place, slot_weighted, precision=highest)
        placed_weights = jnp.einsum("bs,sij->bij", place, slot_weights, precision=highest)
        if weighted is None:
            weighted, weights = placed_weighted, placed_weights
        else:
            weighted, weights = weighted + placed_weighted, weights + placed_weights
    if n_view == 2:
        numer, denom = swap_halves(weighted), swap_halves(weights)
    else:
        numer, denom = (
            lax.psum_scatter(weighted, "view", scatter_dimension=1, tiled=True),
            lax.psum_scatter(weights, "view", scatter_dimension=1, tiled=True),
        )
    return numer / jnp.maximum(denom, 1.0)


def solution(mesh):
    placed = (
        P("view", "brick", None),
        P(None, "view", "brick"),
        P("view", "brick", None, None),
        P("view", "brick"),
    )
    return jax.shard_map(
        functools.partial(local, mesh.shape["view"]), mesh=mesh, in_specs=placed, out_specs=P("brick", "view", None), check_vma=False
    )
```

```python
import functools

import jax
import jax.numpy as jnp
from jax import lax
from jax.sharding import PartitionSpec as P

BS = 128
BLUR = 4
SMOOTH = 4
BRICKS_DEV = 28
WIN = 144
EDGE = 160
LANES = 128


def blur_matrix(out_len, radius):
    out_index = jnp.arange(out_len)[:, None]
    in_index = jnp.arange(out_len + 2 * radius)[None, :]
    offset = (in_index - out_index - radius).astype(jnp.float32)
    spread_px = radius / 2.0
    tap_values = jnp.exp(-offset * offset / (2.0 * spread_px * spread_px))
    tap_line = jnp.arange(-radius, radius + 1).astype(jnp.float32)
    tap_sum = jnp.sum(jnp.exp(-tap_line * tap_line / (2.0 * spread_px * spread_px)))
    inside = jnp.abs(offset) <= radius
    return jnp.where(inside, tap_values / tap_sum, jnp.zeros_like(tap_values))


def contrast(windows):
    inner_len = WIN - 2 * BLUR
    exact = lax.Precision.HIGHEST
    highest = lax.Precision.HIGH
    first_blur = blur_matrix(inner_len, BLUR)
    second_blur = blur_matrix(BS, SMOOTH)
    row_pass = jnp.einsum("ow,nwv->nov", first_blur, windows, precision=exact)
    local_mean = jnp.einsum("nov,pv->nop", row_pass, first_blur, precision=exact)
    inner_part = windows[:, BLUR : BLUR + inner_len, BLUR : BLUR + inner_len]
    energy = (inner_part - local_mean) ** 2
    row_two = jnp.einsum("ow,nwv->nov", second_blur, energy, precision=highest)
    weight = jnp.einsum("nov,pv->nop", row_two, second_blur, precision=highest)
    margin = BLUR + SMOOTH
    center = windows[:, margin : margin + BS, margin : margin + BS]
    return (weight * center, weight)


def cut_windows(square, shift_row, shift_col):
    highest = lax.Precision.HIGHEST
    span = jnp.arange(WIN)[None, :, None]
    cells = jnp.arange(EDGE)[None, None, :]
    pick_rows = (span + shift_row[:, None, None] == cells).astype(jnp.float32)
    pick_cols = (span + shift_col[:, None, None] == cells).astype(jnp.float32)
    rows_cut = jnp.einsum("nie,nef->nif", pick_rows, square, precision=highest)
    return jnp.einsum("nif,njf->nij", rows_cut, pick_cols, precision=highest)


def arrange_slots(arrived, labels):
    flat_slots = arrived.reshape((-1,) + arrived.shape[2:])
    label_ids = labels.reshape(-1).astype(jnp.int32)
    matches = (label_ids[:, None] == jnp.arange(BRICKS_DEV)[None, :]).astype(jnp.int32)
    slot_of = jnp.argmax(matches, axis=0)
    present = jnp.max(matches, axis=0).astype(jnp.float32)
    return flat_slots[slot_of] * present[:, None, None]


def swap_halves(part):
    me = lax.axis_index("view")
    halves = part.reshape(part.shape[0], 2, part.shape[1] // 2, part.shape[2])
    kept = lax.dynamic_index_in_dim(halves, me, axis=1, keepdims=False)
    outgoing = lax.dynamic_index_in_dim(halves, 1 - me, axis=1, keepdims=False)
    arrived = lax.ppermute(outgoing, "view", perm=[(0, 1), (1, 0)])
    return kept + arrived


def local(n_view, tiles, shifts, footprint, target):
    count = tiles.shape[1]
    flat = lax.optimization_barrier(tiles.reshape(count, EDGE * EDGE // LANES, LANES))
    square = flat.reshape(count, EDGE, EDGE)
    windows = cut_windows(square, shifts[0, 0], shifts[1, 0])
    slot_list = footprint[0, 0]
    filled = slot_list >= 0
    picked = jnp.maximum(slot_list, 0)
    labels = jnp.where(filled, target[0][picked], -1).astype(jnp.float32)
    owners, cap = slot_list.shape
    dense_rows = WIN * WIN // LANES
    bricks = jnp.arange(BRICKS_DEV)
    dense_windows = windows.reshape(windows.shape[0], dense_rows, LANES)
    weighted = weights = None
    label_rows = jnp.broadcast_to(labels[:, :, None], (owners, cap, LANES))
    for slot in range(cap):
        mask = filled[:, slot].astype(jnp.float32)[:, None, None]
        packed = dense_windows[picked[:, slot]] * mask
        if slot == 0:
            payload = jnp.concatenate([packed, label_rows], axis=1)
        else:
            payload = packed
        arrived = lax.all_to_all(payload, "brick", split_axis=0, concat_axis=0, tiled=True)
        if weighted is not None:
            weighted, weights, arrived = lax.optimization_barrier((weighted, weights, arrived))
        if slot == 0:
            all_labels = arrived[:, dense_rows:, 0].astype(jnp.int32)
        arrived_labels = all_labels[:, slot]
        slots = arrived[:, :dense_rows].reshape(owners, WIN, WIN)
        slot_weighted, slot_weights = contrast(slots)
        place = (arrived_labels[None, :] == bricks[:, None]).astype(jnp.float32)
        highest = lax.Precision.HIGH
        placed_weighted = jnp.einsum("bs,sij->bij", place, slot_weighted, precision=highest)
        placed_weights = jnp.einsum("bs,sij->bij", place, slot_weights, precision=highest)
        if weighted is None:
            weighted, weights = placed_weighted, placed_weights
        else:
            weighted, weights = weighted + placed_weighted, weights + placed_weights
    if n_view == 2:
        numer, denom = swap_halves(weighted), swap_halves(weights)
    else:
        numer, denom = (
            lax.psum_scatter(weighted, "view", scatter_dimension=1, tiled=True),
            lax.psum_scatter(weights, "view", scatter_dimension=1, tiled=True),
        )
    return numer / jnp.maximum(denom, 1.0)


def solution(mesh):
    placed = (
        P("view", "brick", None),
        P(None, "view", "brick"),
        P("view", "brick", None, None),
        P("view", "brick"),
    )
    return jax.shard_map(
        functools.partial(local, mesh.shape["view"]), mesh=mesh, in_specs=placed, out_specs=P("brick", "view", None), check_vma=False
    )
```

```python
import functools

import jax
import jax.numpy as jnp
from jax import lax
from jax.sharding import PartitionSpec as P

BS = 128
BLUR = 4
SMOOTH = 4
BRICKS_DEV = 28
WIN = 144
EDGE = 160
LANES = 128


def blur_matrix(out_len, radius):
    out_index = jnp.arange(out_len)[:, None]
    in_index = jnp.arange(out_len + 2 * radius)[None, :]
    offset = (in_index - out_index - radius).astype(jnp.float32)
    spread_px = radius / 2.0
    tap_values = jnp.exp(-offset * offset / (2.0 * spread_px * spread_px))
    tap_line = jnp.arange(-radius, radius + 1).astype(jnp.float32)
    tap_sum = jnp.sum(jnp.exp(-tap_line * tap_line / (2.0 * spread_px * spread_px)))
    inside = jnp.abs(offset) <= radius
    return jnp.where(inside, tap_values / tap_sum, jnp.zeros_like(tap_values))


def contrast(windows):
    inner_len = WIN - 2 * BLUR
    exact = lax.Precision.HIGHEST
    highest = lax.Precision.HIGH
    first_blur = blur_matrix(inner_len, BLUR)
    second_blur = blur_matrix(BS, SMOOTH)
    row_pass = jnp.einsum("ow,nwv->nov", first_blur, windows, precision=exact)
    local_mean = jnp.einsum("nov,pv->nop", row_pass, first_blur, precision=exact)
    inner_part = windows[:, BLUR : BLUR + inner_len, BLUR : BLUR + inner_len]
    energy = (inner_part - local_mean) ** 2
    row_two = jnp.einsum("ow,nwv->nov", second_blur, energy, precision=highest)
    weight = jnp.einsum("nov,pv->nop", row_two, second_blur, precision=highest)
    margin = BLUR + SMOOTH
    center = windows[:, margin : margin + BS, margin : margin + BS]
    return (weight * center, weight)


def cut_windows(square, shift_row, shift_col):
    highest = lax.Precision.HIGHEST
    span = jnp.arange(WIN)[None, :, None]
    cells = jnp.arange(EDGE)[None, None, :]
    pick_rows = (span + shift_row[:, None, None] == cells).astype(jnp.float32)
    pick_cols = (span + shift_col[:, None, None] == cells).astype(jnp.float32)
    rows_cut = jnp.einsum("nie,nef->nif", pick_rows, square, precision=highest)
    return jnp.einsum("nif,njf->nij", rows_cut, pick_cols, precision=highest)


def arrange_slots(arrived, labels):
    flat_slots = arrived.reshape((-1,) + arrived.shape[2:])
    label_ids = labels.reshape(-1).astype(jnp.int32)
    matches = (label_ids[:, None] == jnp.arange(BRICKS_DEV)[None, :]).astype(jnp.int32)
    slot_of = jnp.argmax(matches, axis=0)
    present = jnp.max(matches, axis=0).astype(jnp.float32)
    return flat_slots[slot_of] * present[:, None, None]


def swap_halves(part):
    me = lax.axis_index("view")
    halves = part.reshape(part.shape[0], 2, part.shape[1] // 2, part.shape[2])
    kept = lax.dynamic_index_in_dim(halves, me, axis=1, keepdims=False)
    outgoing = lax.dynamic_index_in_dim(halves, 1 - me, axis=1, keepdims=False)
    arrived = lax.ppermute(outgoing, "view", perm=[(0, 1), (1, 0)])
    return kept + arrived


def local(n_view, tiles, shifts, footprint, target):
    count = tiles.shape[1]
    flat = lax.optimization_barrier(tiles.reshape(count, EDGE * EDGE // LANES, LANES))
    square = flat.reshape(count, EDGE, EDGE)
    windows = cut_windows(square, shifts[0, 0], shifts[1, 0])
    slot_list = footprint[0, 0]
    filled = slot_list >= 0
    picked = jnp.maximum(slot_list, 0)
    listed = slot_list[:, :, None] == jnp.arange(count)[None, None, :]
    labels = jnp.sum(jnp.where(listed, target[0][None, None, :], 0), axis=2)
    labels = jnp.where(filled, labels, -1).astype(jnp.float32)
    owners, cap = slot_list.shape
    dense_rows = WIN * WIN // LANES
    bricks = jnp.arange(BRICKS_DEV)
    dense_windows = windows.reshape(windows.shape[0], dense_rows, LANES)
    weighted = weights = None
    label_rows = jnp.broadcast_to(labels[:, :, None], (owners, cap, LANES))
    for slot in range(cap):
        packed = dense_windows[picked[:, slot]]
        if slot == 0:
            payload = jnp.concatenate([packed, label_rows], axis=1)
        else:
            payload = packed
        arrived = lax.all_to_all(payload, "brick", split_axis=0, concat_axis=0, tiled=True)
        if weighted is not None:
            weighted, weights, arrived = lax.optimization_barrier((weighted, weights, arrived))
        if slot == 0:
            all_labels = arrived[:, dense_rows:, 0].astype(jnp.int32)
        arrived_labels = all_labels[:, slot]
        slots = arrived[:, :dense_rows].reshape(owners, WIN, WIN)
        slot_weighted, slot_weights = contrast(slots)
        place = (arrived_labels[None, :] == bricks[:, None]).astype(jnp.float32)
        highest = lax.Precision.HIGH
        placed_weighted = jnp.einsum("bs,sij->bij", place, slot_weighted, precision=highest)
        placed_weights = jnp.einsum("bs,sij->bij", place, slot_weights, precision=highest)
        if weighted is None:
            weighted, weights = placed_weighted, placed_weights
        else:
            weighted, weights = weighted + placed_weighted, weights + placed_weights
    if n_view == 2:
        numer, denom = swap_halves(weighted), swap_halves(weights)
    else:
        numer, denom = (
            lax.psum_scatter(weighted, "view", scatter_dimension=1, tiled=True),
            lax.psum_scatter(weights, "view", scatter_dimension=1, tiled=True),
        )
    return numer / jnp.maximum(denom, 1.0)


def solution(mesh):
    placed = (
        P("view", "brick", None),
        P(None, "view", "brick"),
        P("view", "brick", None, None),
        P("view", "brick"),
    )
    return jax.shard_map(
        functools.partial(local, mesh.shape["view"]), mesh=mesh, in_specs=placed, out_specs=P("brick", "view", None), check_vma=False
    )
```

```python
import functools

import jax
import jax.numpy as jnp
from jax import lax
from jax.sharding import PartitionSpec as P

BS = 128
BLUR = 4
SMOOTH = 4
BRICKS_DEV = 28
WIN = 144
EDGE = 160
LANES = 128


def blur_matrix(out_len, radius):
    out_index = jnp.arange(out_len)[:, None]
    in_index = jnp.arange(out_len + 2 * radius)[None, :]
    offset = (in_index - out_index - radius).astype(jnp.float32)
    spread_px = radius / 2.0
    tap_values = jnp.exp(-offset * offset / (2.0 * spread_px * spread_px))
    tap_line = jnp.arange(-radius, radius + 1).astype(jnp.float32)
    tap_sum = jnp.sum(jnp.exp(-tap_line * tap_line / (2.0 * spread_px * spread_px)))
    inside = jnp.abs(offset) <= radius
    return jnp.where(inside, tap_values / tap_sum, jnp.zeros_like(tap_values))


def blur_taps(radius):
    line = jnp.arange(-radius, radius + 1).astype(jnp.float32)
    spread = radius / 2.0
    values = jnp.exp(-line * line / (2.0 * spread * spread))
    return values / jnp.sum(values)


def tap_rows(x, taps, out_len):
    total = taps[0] * x[:, 0:out_len, :]
    for k in range(1, taps.shape[0]):
        total = total + taps[k] * x[:, k : k + out_len, :]
    return total


def tap_cols(x, taps, out_len):
    total = taps[0] * x[:, :, 0:out_len]
    for k in range(1, taps.shape[0]):
        total = total + taps[k] * x[:, :, k : k + out_len]
    return total


def contrast(windows):
    inner_len = WIN - 2 * BLUR
    first_taps = blur_taps(BLUR)
    second_taps = blur_taps(SMOOTH)
    row_pass = lax.optimization_barrier(tap_rows(windows, first_taps, inner_len))
    local_mean = tap_cols(row_pass, first_taps, inner_len)
    inner_part = windows[:, BLUR : BLUR + inner_len, BLUR : BLUR + inner_len]
    energy = (inner_part - local_mean) ** 2
    row_two = lax.optimization_barrier(tap_rows(energy, second_taps, BS))
    weight = tap_cols(row_two, second_taps, BS)
    margin = BLUR + SMOOTH
    center = windows[:, margin : margin + BS, margin : margin + BS]
    return (weight * center, weight)


def cut_windows(square, shift_row, shift_col):
    highest = lax.Precision.HIGHEST
    span = jnp.arange(WIN)[None, :, None]
    cells = jnp.arange(EDGE)[None, None, :]
    pick_rows = (span + shift_row[:, None, None] == cells).astype(jnp.float32)
    pick_cols = (span + shift_col[:, None, None] == cells).astype(jnp.float32)
    rows_cut = jnp.einsum("nie,nef->nif", pick_rows, square, precision=highest)
    return jnp.einsum("nif,njf->nij", rows_cut, pick_cols, precision=highest)


def arrange_slots(arrived, labels):
    flat_slots = arrived.reshape((-1,) + arrived.shape[2:])
    label_ids = labels.reshape(-1).astype(jnp.int32)
    matches = (label_ids[:, None] == jnp.arange(BRICKS_DEV)[None, :]).astype(jnp.int32)
    slot_of = jnp.argmax(matches, axis=0)
    present = jnp.max(matches, axis=0).astype(jnp.float32)
    return flat_slots[slot_of] * present[:, None, None]


def swap_halves(part):
    me = lax.axis_index("view")
    halves = part.reshape(part.shape[0], 2, part.shape[1] // 2, part.shape[2])
    kept = lax.dynamic_index_in_dim(halves, me, axis=1, keepdims=False)
    outgoing = lax.dynamic_index_in_dim(halves, 1 - me, axis=1, keepdims=False)
    arrived = lax.ppermute(outgoing, "view", perm=[(0, 1), (1, 0)])
    return kept + arrived


def local(n_view, tiles, shifts, footprint, target):
    count = tiles.shape[1]
    flat = lax.optimization_barrier(tiles.reshape(count, EDGE * EDGE // LANES, LANES))
    square = flat.reshape(count, EDGE, EDGE)
    windows = cut_windows(square, shifts[0, 0], shifts[1, 0])
    slot_list = footprint[0, 0]
    filled = slot_list >= 0
    picked = jnp.maximum(slot_list, 0)
    listed = slot_list[:, :, None] == jnp.arange(count)[None, None, :]
    labels = jnp.sum(jnp.where(listed, target[0][None, None, :], 0), axis=2)
    labels = jnp.where(filled, labels, -1).astype(jnp.float32)
    owners, cap = slot_list.shape
    dense_rows = WIN * WIN // LANES
    bricks = jnp.arange(BRICKS_DEV)
    dense_windows = windows.reshape(windows.shape[0], dense_rows, LANES)
    weighted = weights = None
    label_rows = jnp.broadcast_to(labels[:, :, None], (owners, cap, LANES))
    for slot in range(cap):
        packed = dense_windows[picked[:, slot]]
        if slot == 0:
            payload = jnp.concatenate([packed, label_rows], axis=1)
        else:
            payload = packed
        arrived = lax.all_to_all(payload, "brick", split_axis=0, concat_axis=0, tiled=True)
        if weighted is not None:
            weighted, weights, arrived = lax.optimization_barrier((weighted, weights, arrived))
        if slot == 0:
            all_labels = arrived[:, dense_rows:, 0].astype(jnp.int32)
        arrived_labels = all_labels[:, slot]
        slots = arrived[:, :dense_rows].reshape(owners, WIN, WIN)
        slot_weighted, slot_weights = contrast(slots)
        place = (arrived_labels[None, :] == bricks[:, None]).astype(jnp.float32)
        highest = lax.Precision.HIGH
        placed_weighted = jnp.einsum("bs,sij->bij", place, slot_weighted, precision=highest)
        placed_weights = jnp.einsum("bs,sij->bij", place, slot_weights, precision=highest)
        if weighted is None:
            weighted, weights = placed_weighted, placed_weights
        else:
            weighted, weights = weighted + placed_weighted, weights + placed_weights
    if n_view == 2:
        numer, denom = swap_halves(weighted), swap_halves(weights)
    else:
        numer, denom = (
            lax.psum_scatter(weighted, "view", scatter_dimension=1, tiled=True),
            lax.psum_scatter(weights, "view", scatter_dimension=1, tiled=True),
        )
    return numer / jnp.maximum(denom, 1.0)


def solution(mesh):
    placed = (
        P("view", "brick", None),
        P(None, "view", "brick"),
        P("view", "brick", None, None),
        P("view", "brick"),
    )
    return jax.shard_map(
        functools.partial(local, mesh.shape["view"]), mesh=mesh, in_specs=placed, out_specs=P("brick", "view", None), check_vma=False
    )
```

```python
import functools

import jax
import jax.numpy as jnp
from jax import lax
from jax.sharding import PartitionSpec as P

BS = 128
BLUR = 4
SMOOTH = 4
BRICKS_DEV = 28
WIN = 144
EDGE = 160
LANES = 128


def blur_matrix(out_len, radius):
    out_index = jnp.arange(out_len)[:, None]
    in_index = jnp.arange(out_len + 2 * radius)[None, :]
    offset = (in_index - out_index - radius).astype(jnp.float32)
    spread_px = radius / 2.0
    tap_values = jnp.exp(-offset * offset / (2.0 * spread_px * spread_px))
    tap_line = jnp.arange(-radius, radius + 1).astype(jnp.float32)
    tap_sum = jnp.sum(jnp.exp(-tap_line * tap_line / (2.0 * spread_px * spread_px)))
    inside = jnp.abs(offset) <= radius
    return jnp.where(inside, tap_values / tap_sum, jnp.zeros_like(tap_values))


def contrast(windows):
    inner_len = WIN - 2 * BLUR
    exact = lax.Precision.HIGHEST
    highest = lax.Precision.HIGH
    first_blur = blur_matrix(inner_len, BLUR)
    second_blur = blur_matrix(BS, SMOOTH)
    row_pass = jnp.einsum("ow,nwv->nov", first_blur, windows, precision=exact)
    local_mean = jnp.einsum("nov,pv->nop", row_pass, first_blur, precision=exact)
    inner_part = windows[:, BLUR : BLUR + inner_len, BLUR : BLUR + inner_len]
    energy = (inner_part - local_mean) ** 2
    row_two = jnp.einsum("ow,nwv->nov", second_blur, energy, precision=highest)
    weight = jnp.einsum("nov,pv->nop", row_two, second_blur, precision=highest)
    margin = BLUR + SMOOTH
    center = windows[:, margin : margin + BS, margin : margin + BS]
    return (weight * center, weight)


def cut_windows(square, shift_row, shift_col):
    highest = lax.Precision.HIGHEST
    span = jnp.arange(WIN)[None, :, None]
    cells = jnp.arange(EDGE)[None, None, :]
    pick_rows = (span + shift_row[:, None, None] == cells).astype(jnp.float32)
    pick_cols = (span + shift_col[:, None, None] == cells).astype(jnp.float32)
    rows_cut = jnp.einsum("nie,nef->nif", pick_rows, square, precision=highest)
    return jnp.einsum("nif,njf->nij", rows_cut, pick_cols, precision=highest)


def arrange_slots(arrived, labels):
    flat_slots = arrived.reshape((-1,) + arrived.shape[2:])
    label_ids = labels.reshape(-1).astype(jnp.int32)
    matches = (label_ids[:, None] == jnp.arange(BRICKS_DEV)[None, :]).astype(jnp.int32)
    slot_of = jnp.argmax(matches, axis=0)
    present = jnp.max(matches, axis=0).astype(jnp.float32)
    return flat_slots[slot_of] * present[:, None, None]


def swap_halves(part):
    me = lax.axis_index("view")
    halves = part.reshape(part.shape[0], 2, part.shape[1] // 2, part.shape[2])
    kept = lax.dynamic_index_in_dim(halves, me, axis=1, keepdims=False)
    outgoing = lax.dynamic_index_in_dim(halves, 1 - me, axis=1, keepdims=False)
    arrived = lax.ppermute(outgoing, "view", perm=[(0, 1), (1, 0)])
    return kept + arrived


def local(n_view, tiles, shifts, footprint, target):
    count = tiles.shape[1]
    flat = lax.optimization_barrier(tiles.reshape(count, EDGE * EDGE // LANES, LANES))
    square = flat.reshape(count, EDGE, EDGE)
    windows = cut_windows(square, shifts[0, 0], shifts[1, 0])
    slot_list = footprint[0, 0]
    filled = slot_list >= 0
    picked = jnp.maximum(slot_list, 0)
    listed = slot_list[:, :, None] == jnp.arange(count)[None, None, :]
    labels = jnp.sum(jnp.where(listed, target[0][None, None, :], 0), axis=2)
    labels = jnp.where(filled, labels, -1).astype(jnp.float32)
    owners, cap = slot_list.shape
    dense_rows = WIN * WIN // LANES
    bricks = jnp.arange(BRICKS_DEV)
    dense_windows = windows.reshape(windows.shape[0], dense_rows, LANES)
    weighted = weights = None
    label_rows = jnp.broadcast_to(labels[:, :, None], (owners, cap, LANES))
    for slot in range(cap):
        packed = dense_windows[picked[:, slot]]
        if slot == 0:
            payload = jnp.concatenate([packed, label_rows], axis=1)
        else:
            payload = packed
        aligned = -(-payload.shape[1] // 8) * 8
        payload = jnp.pad(payload, ((0, 0), (0, aligned - payload.shape[1]), (0, 0)))
        arrived = lax.all_to_all(payload, "brick", split_axis=0, concat_axis=0, tiled=True)
        if weighted is not None:
            weighted, weights, arrived = lax.optimization_barrier((weighted, weights, arrived))
        if slot == 0:
            all_labels = arrived[:, dense_rows : dense_rows + cap, 0].astype(jnp.int32)
        arrived_labels = all_labels[:, slot]
        slots = arrived[:, :dense_rows].reshape(owners, WIN, WIN)
        slot_weighted, slot_weights = contrast(slots)
        place = (arrived_labels[None, :] == bricks[:, None]).astype(jnp.float32)
        highest = lax.Precision.HIGH
        placed_weighted = jnp.einsum("bs,sij->bij", place, slot_weighted, precision=highest)
        placed_weights = jnp.einsum("bs,sij->bij", place, slot_weights, precision=highest)
        if weighted is None:
            weighted, weights = placed_weighted, placed_weights
        else:
            weighted, weights = weighted + placed_weighted, weights + placed_weights
    if n_view == 2:
        numer, denom = swap_halves(weighted), swap_halves(weights)
    else:
        numer, denom = (
            lax.psum_scatter(weighted, "view", scatter_dimension=1, tiled=True),
            lax.psum_scatter(weights, "view", scatter_dimension=1, tiled=True),
        )
    return numer / jnp.maximum(denom, 1.0)


def solution(mesh):
    placed = (
        P("view", "brick", None),
        P(None, "view", "brick"),
        P("view", "brick", None, None),
        P("view", "brick"),
    )
    return jax.shard_map(
        functools.partial(local, mesh.shape["view"]), mesh=mesh, in_specs=placed, out_specs=P("brick", "view", None), check_vma=False
    )
```

```python
import functools

import jax
import jax.numpy as jnp
from jax import lax
from jax.sharding import PartitionSpec as P

BS = 128
BLUR = 4
SMOOTH = 4
BRICKS_DEV = 28
WIN = 144
EDGE = 160
LANES = 128


def blur_matrix(out_len, radius):
    out_index = jnp.arange(out_len)[:, None]
    in_index = jnp.arange(out_len + 2 * radius)[None, :]
    offset = (in_index - out_index - radius).astype(jnp.float32)
    spread_px = radius / 2.0
    tap_values = jnp.exp(-offset * offset / (2.0 * spread_px * spread_px))
    tap_line = jnp.arange(-radius, radius + 1).astype(jnp.float32)
    tap_sum = jnp.sum(jnp.exp(-tap_line * tap_line / (2.0 * spread_px * spread_px)))
    inside = jnp.abs(offset) <= radius
    return jnp.where(inside, tap_values / tap_sum, jnp.zeros_like(tap_values))


def contrast(windows):
    inner_len = WIN - 2 * BLUR
    exact = lax.Precision.HIGHEST
    highest = lax.Precision.HIGH
    first_blur = blur_matrix(inner_len, BLUR)
    second_blur = blur_matrix(BS, SMOOTH)
    row_pass = jnp.einsum("ow,nwv->nov", first_blur, windows, precision=exact)
    local_mean = jnp.einsum("nov,pv->nop", row_pass, first_blur, precision=exact)
    inner_part = windows[:, BLUR : BLUR + inner_len, BLUR : BLUR + inner_len]
    energy = (inner_part - local_mean) ** 2
    row_two = jnp.einsum("ow,nwv->nov", second_blur, energy, precision=highest)
    weight = jnp.einsum("nov,pv->nop", row_two, second_blur, precision=highest)
    margin = BLUR + SMOOTH
    center = windows[:, margin : margin + BS, margin : margin + BS]
    return (weight * center, weight)


def cut_windows(square, shift_row, shift_col):
    highest = lax.Precision.HIGHEST
    span = jnp.arange(WIN)[None, :, None]
    cells = jnp.arange(EDGE)[None, None, :]
    pick_rows = (span + shift_row[:, None, None] == cells).astype(jnp.float32)
    pick_cols = (span + shift_col[:, None, None] == cells).astype(jnp.float32)
    rows_cut = jnp.einsum("nie,nef->nif", pick_rows, square, precision=highest)
    return jnp.einsum("nif,njf->nij", rows_cut, pick_cols, precision=highest)


def arrange_slots(arrived, labels):
    flat_slots = arrived.reshape((-1,) + arrived.shape[2:])
    label_ids = labels.reshape(-1).astype(jnp.int32)
    matches = (label_ids[:, None] == jnp.arange(BRICKS_DEV)[None, :]).astype(jnp.int32)
    slot_of = jnp.argmax(matches, axis=0)
    present = jnp.max(matches, axis=0).astype(jnp.float32)
    return flat_slots[slot_of] * present[:, None, None]


def swap_halves(part):
    me = lax.axis_index("view")
    halves = part.reshape(part.shape[0], 2, part.shape[1] // 2, part.shape[2])
    kept = lax.dynamic_index_in_dim(halves, me, axis=1, keepdims=False)
    outgoing = lax.dynamic_index_in_dim(halves, 1 - me, axis=1, keepdims=False)
    arrived = lax.ppermute(outgoing, "view", perm=[(0, 1), (1, 0)])
    return kept + arrived


def local(n_view, tiles, shifts, footprint, target):
    count = tiles.shape[1]
    flat = lax.optimization_barrier(tiles.reshape(count, EDGE * EDGE // LANES, LANES))
    square = flat.reshape(count, EDGE, EDGE)
    windows = cut_windows(square, shifts[0, 0], shifts[1, 0])
    slot_list = footprint[0, 0]
    filled = slot_list >= 0
    picked = jnp.maximum(slot_list, 0)
    listed = slot_list[:, :, None] == jnp.arange(count)[None, None, :]
    labels = jnp.sum(jnp.where(listed, target[0][None, None, :], 0), axis=2)
    labels = jnp.where(filled, labels, -1).astype(jnp.float32)
    owners, cap = slot_list.shape
    dense_rows = WIN * WIN // LANES
    bricks = jnp.arange(BRICKS_DEV)
    dense_windows = windows.reshape(windows.shape[0], dense_rows, LANES)
    weighted = weights = None
    label_rows = jnp.broadcast_to(labels[:, :, None], (owners, cap, LANES))
    for slot in range(cap):
        packed = dense_windows[picked[:, slot]]
        if slot == 0:
            payload = jnp.concatenate([packed, label_rows], axis=1)
        else:
            payload = packed
        arrived = lax.all_to_all(payload, "brick", split_axis=0, concat_axis=0, tiled=True)
        if weighted is not None:
            weighted, weights, arrived = lax.optimization_barrier((weighted, weights, arrived))
        if slot == 0:
            all_labels = arrived[:, dense_rows:, 0].astype(jnp.int32)
        arrived_labels = all_labels[:, slot]
        slots = arrived[:, :dense_rows].reshape(owners, WIN, WIN)
        slot_weighted, slot_weights = contrast(slots)
        place = (arrived_labels[None, :] == bricks[:, None]).astype(jnp.float32)
        highest = lax.Precision.HIGH
        placed_weighted = jnp.einsum("bs,sij->bij", place, slot_weighted, precision=highest)
        placed_weights = jnp.einsum("bs,sij->bij", place, slot_weights, precision=highest)
        if weighted is None:
            weighted, weights = placed_weighted, placed_weights
        else:
            weighted, weights = weighted + placed_weighted, weights + placed_weights
    if n_view == 2:
        scale = lax.optimization_barrier(jnp.maximum(swap_halves(weights), 1.0))
        return swap_halves(weighted) / scale
    else:
        numer, denom = (
            lax.psum_scatter(weighted, "view", scatter_dimension=1, tiled=True),
            lax.psum_scatter(weights, "view", scatter_dimension=1, tiled=True),
        )
    return numer / jnp.maximum(denom, 1.0)


def solution(mesh):
    placed = (
        P("view", "brick", None),
        P(None, "view", "brick"),
        P("view", "brick", None, None),
        P("view", "brick"),
    )
    return jax.shard_map(
        functools.partial(local, mesh.shape["view"]), mesh=mesh, in_specs=placed, out_specs=P("brick", "view", None), check_vma=False
    )
```

```python
import functools

import jax
import jax.numpy as jnp
from jax import lax
from jax.sharding import PartitionSpec as P

BS = 128
BLUR = 4
SMOOTH = 4
BRICKS_DEV = 28
WIN = 144
EDGE = 160
LANES = 128


def blur_matrix(out_len, radius):
    out_index = jnp.arange(out_len)[:, None]
    in_index = jnp.arange(out_len + 2 * radius)[None, :]
    offset = (in_index - out_index - radius).astype(jnp.float32)
    spread_px = radius / 2.0
    tap_values = jnp.exp(-offset * offset / (2.0 * spread_px * spread_px))
    tap_line = jnp.arange(-radius, radius + 1).astype(jnp.float32)
    tap_sum = jnp.sum(jnp.exp(-tap_line * tap_line / (2.0 * spread_px * spread_px)))
    inside = jnp.abs(offset) <= radius
    return jnp.where(inside, tap_values / tap_sum, jnp.zeros_like(tap_values))


def contrast(slab):
    exact = lax.Precision.HIGHEST
    highest = lax.Precision.HIGH
    inner_rows = slab.shape[1] - 2 * BLUR
    out_rows = inner_rows - 2 * SMOOTH
    inner_len = WIN - 2 * BLUR
    first_rows = blur_matrix(inner_rows, BLUR)
    first_cols = blur_matrix(inner_len, BLUR)
    second_rows = blur_matrix(out_rows, SMOOTH)
    second_cols = blur_matrix(BS, SMOOTH)
    row_pass = jnp.einsum("ow,nwv->nov", first_rows, slab, precision=exact)
    local_mean = jnp.einsum("nov,pv->nop", row_pass, first_cols, precision=exact)
    inner_part = slab[:, BLUR : BLUR + inner_rows, BLUR : BLUR + inner_len]
    energy = (inner_part - local_mean) ** 2
    row_two = jnp.einsum("ow,nwv->nov", second_rows, energy, precision=highest)
    weight = jnp.einsum("nov,pv->nop", row_two, second_cols, precision=highest)
    margin = BLUR + SMOOTH
    center = slab[:, margin : margin + out_rows, margin : margin + BS]
    return (weight * center, weight)


def cut_windows(square, shift_row, shift_col):
    highest = lax.Precision.HIGHEST
    span = jnp.arange(WIN)[None, :, None]
    cells = jnp.arange(EDGE)[None, None, :]
    pick_rows = (span + shift_row[:, None, None] == cells).astype(jnp.float32)
    pick_cols = (span + shift_col[:, None, None] == cells).astype(jnp.float32)
    rows_cut = jnp.einsum("nie,nef->nif", pick_rows, square, precision=highest)
    return jnp.einsum("nif,njf->nij", rows_cut, pick_cols, precision=highest)


def arrange_slots(arrived, labels):
    flat_slots = arrived.reshape((-1,) + arrived.shape[2:])
    label_ids = labels.reshape(-1).astype(jnp.int32)
    matches = (label_ids[:, None] == jnp.arange(BRICKS_DEV)[None, :]).astype(jnp.int32)
    slot_of = jnp.argmax(matches, axis=0)
    present = jnp.max(matches, axis=0).astype(jnp.float32)
    return flat_slots[slot_of] * present[:, None, None]


def swap_halves(part):
    me = lax.axis_index("view")
    halves = part.reshape(part.shape[0], 2, part.shape[1] // 2, part.shape[2])
    kept = lax.dynamic_index_in_dim(halves, me, axis=1, keepdims=False)
    outgoing = lax.dynamic_index_in_dim(halves, 1 - me, axis=1, keepdims=False)
    arrived = lax.ppermute(outgoing, "view", perm=[(0, 1), (1, 0)])
    return kept + arrived


def local(n_view, tiles, shifts, footprint, target):
    count = tiles.shape[1]
    flat = lax.optimization_barrier(tiles.reshape(count, EDGE * EDGE // LANES, LANES))
    square = flat.reshape(count, EDGE, EDGE)
    windows = cut_windows(square, shifts[0, 0], shifts[1, 0])
    slot_list = footprint[0, 0]
    filled = slot_list >= 0
    picked = jnp.maximum(slot_list, 0)
    listed = slot_list[:, :, None] == jnp.arange(count)[None, None, :]
    labels = jnp.sum(jnp.where(listed, target[0][None, None, :], 0), axis=2)
    labels = jnp.where(filled, labels, -1).astype(jnp.float32)
    owners, cap = slot_list.shape
    dense_rows = WIN * WIN // LANES
    bricks = jnp.arange(BRICKS_DEV)
    dense_windows = windows.reshape(windows.shape[0], dense_rows, LANES)
    weighted = weights = None
    label_rows = jnp.broadcast_to(labels[:, :, None], (owners, cap, LANES))
    for slot in range(cap):
        packed = dense_windows[picked[:, slot]]
        if slot == 0:
            payload = jnp.concatenate([packed, label_rows], axis=1)
        else:
            payload = packed
        arrived = lax.all_to_all(payload, "brick", split_axis=0, concat_axis=0, tiled=True)
        if weighted is not None:
            weighted, weights, arrived = lax.optimization_barrier((weighted, weights, arrived))
        if slot == 0:
            all_labels = arrived[:, dense_rows:, 0].astype(jnp.int32)
        arrived_labels = all_labels[:, slot]
        place = (arrived_labels[None, :] == bricks[:, None]).astype(jnp.float32)
        highest = lax.Precision.HIGH
        if n_view == 2 and slot == cap - 1:
            me = lax.axis_index("view")
            pair = [(0, 1), (1, 0)]
            slab_rows = BS // 2 + 2 * (BLUR + SMOOTH)
            slab_dense = slab_rows * WIN // LANES
            offset = dense_rows - slab_dense
            kept = lax.dynamic_slice_in_dim(arrived, me * offset, slab_dense, axis=1)
            outgoing = lax.dynamic_slice_in_dim(arrived, (1 - me) * offset, slab_dense, axis=1)
            received = lax.ppermute(outgoing, "view", perm=pair)
            other_labels = lax.ppermute(arrived_labels, "view", perm=pair)
            other_place = (other_labels[None, :] == bricks[:, None]).astype(jnp.float32)
            own_weighted, own_weights = contrast(kept.reshape(owners, slab_rows, WIN))
            far_weighted, far_weights = contrast(received.reshape(owners, slab_rows, WIN))
            placed_weighted = jnp.einsum("bs,sij->bij", place, own_weighted, precision=highest)
            placed_weighted = placed_weighted + jnp.einsum("bs,sij->bij", other_place, far_weighted, precision=highest)
            placed_weights = jnp.einsum("bs,sij->bij", place, own_weights, precision=highest)
            placed_weights = placed_weights + jnp.einsum("bs,sij->bij", other_place, far_weights, precision=highest)
        else:
            slots = arrived[:, :dense_rows].reshape(owners, WIN, WIN)
            slot_weighted, slot_weights = contrast(slots)
            placed_weighted = jnp.einsum("bs,sij->bij", place, slot_weighted, precision=highest)
            placed_weights = jnp.einsum("bs,sij->bij", place, slot_weights, precision=highest)
            if n_view == 2:
                placed_weighted = swap_halves(placed_weighted)
                placed_weights = swap_halves(placed_weights)
        if weighted is None:
            weighted, weights = placed_weighted, placed_weights
        else:
            weighted, weights = weighted + placed_weighted, weights + placed_weights
    if n_view == 2:
        return weighted / jnp.maximum(weights, 1.0)
    numer, denom = (
        lax.psum_scatter(weighted, "view", scatter_dimension=1, tiled=True),
        lax.psum_scatter(weights, "view", scatter_dimension=1, tiled=True),
    )
    return numer / jnp.maximum(denom, 1.0)


def solution(mesh):
    placed = (
        P("view", "brick", None),
        P(None, "view", "brick"),
        P("view", "brick", None, None),
        P("view", "brick"),
    )
    return jax.shard_map(
        functools.partial(local, mesh.shape["view"]), mesh=mesh, in_specs=placed, out_specs=P("brick", "view", None), check_vma=False
    )
```
